32 devices in a mesh: rep: 4 (over y, core), ep: 8 (over z, x).
Axes of the slice: x: 2, y: 2, z: 4, core: 2. Of those that a mesh axis runs over, the one named last changes fastest.
Arguments:
- tokens: bfloat16 [8192, 2048], P(('rep', 'ep')), may hold values from -6 to 6
- expert_ids: int32 [8192, 8], P(('rep', 'ep')), may hold values from 0 to 127, as said below
- gate_weights: float32 [8192, 8], P(('rep', 'ep')), may hold values from 0.25 to 1
- w_gate: bfloat16 [8, 768, 2048], P('ep'), may hold values from -0.125 to 0.125
- w_up: bfloat16 [8, 768, 2048], P('ep'), may hold values from -0.125 to 0.125
- w_down: bfloat16 [8, 768, 2048], P('ep'), may hold values from -0.21875 to 0.21875
- out_grad: bfloat16 [8192, 2048], P(('rep', 'ep')), may hold values from -6 to 6
Outputs:
- layer_out: bfloat16 [8192, 2048], P(('rep', 'ep'))
- tokens_grad: bfloat16 [8192, 2048], P(('rep', 'ep'))
- gates_grad: float32 [8192, 8], P(('rep', 'ep'))
- gate_w_grad: bfloat16 [8, 768, 2048], P('ep', 'rep')
- up_w_grad: bfloat16 [8, 768, 2048], P('ep', 'rep')
- down_w_grad: bfloat16 [8, 768, 2048], P('ep', 'rep')
The draws below stay inside these ranges and needn't reach their ends.
Inputs may be any that keep to these rules, and one draw needn't show every extreme that they name: `expert_ids`: entry j of a row lies in [16 * j, 16 * j + 16); in the rows of one device no id below 8 appears more than 32 times, and some id below 8 appears exactly 32 times.
All inputs are finite; a program needn't handle non-finite values.
Results may differ from the reference program's by a relative error of at most 0.0065.
Values may be sent and summed in bfloat16 or wider, within the bound.
No kernel may reach another device: no remote copies, remote signals or barrier semaphores. Data moves between devices by JAX's collectives and lax.ppermute only.
A program may use at most 128 MiB of HBM per device.

```python
import math
import jax
import jax.numpy as jnp
from jax import lax

D = 2048
FF = 768
TOP = 8
TOK_DEV = 256
STRIPE = 16
CAP = 32
EXPERTS = 8
TOKENS = 8192


def draw_expert_ids(key, part):
    blocks = TOKENS // TOK_DEV
    key_hot, key_first, key_order = jax.random.split(key, 3)
    hot_value = jax.random.randint(key_hot, (blocks, TOP), 0, STRIPE)
    first_hot = jax.random.randint(key_first, (blocks, 1), 0, min(STRIPE, EXPERTS))
    hot_value = jnp.concatenate([first_hot, hot_value[:, 1:]], axis=1)
    position = jnp.arange(TOK_DEV, dtype=jnp.int32)
    offset = jnp.where(position < CAP, 0, 1 + (position - CAP) % (STRIPE - 1))
    values = (hot_value[:, :, None] + offset[None, None, :]) % STRIPE
    order_keys = jax.random.split(key_order, blocks * TOP)

    def one_order(order_key):
        return jax.random.permutation(order_key, TOK_DEV)
    orders = jax.vmap(one_order)(order_keys).reshape(blocks, TOP, TOK_DEV)
    shuffled = jnp.take_along_axis(values, orders, axis=2)
    stripe_ids = shuffled + STRIPE * jnp.arange(TOP, dtype=jnp.int32)[None, :, None]
    return jnp.transpose(stripe_ids, (0, 2, 1)).reshape(TOKENS, TOP).astype(jnp.int32)


def level_of(stream_key, extent, cuts, least, largest):
    gain, own = 1.0, jax.random.fold_in(stream_key, 6)
    for axis_at, blocks in cuts:
        heights = jnp.exp(jax.random.uniform(jax.random.fold_in(own, axis_at), (blocks,), jnp.float32, least / len(cuts), largest / len(cuts)))
        gain = gain * jnp.repeat(heights, extent[axis_at] // blocks).reshape([-1 if axis == axis_at else 1 for axis in range(len(extent))])
    return gain


def scatter_about(stream_key, shape, scale, most, cuts=(), kind=jnp.bfloat16):
    result = scale * jax.random.normal(stream_key, shape, jnp.float32)
    if cuts:
        result = result * level_of(stream_key, shape, cuts, -0.22, 0.18)
    return jnp.clip(result, -most, most).astype(kind)


def setup_inputs(seed: int = 0) -> dict:
    keys = jax.random.split(jax.random.key(seed), 8)
    tokens = scatter_about(keys[0], (TOKENS, D), 1.0, 6.0, ((0, 32),))
    expert_ids = draw_expert_ids(jax.random.fold_in(keys[7], 71), 0)
    gate_weights = jnp.clip(jnp.exp(math.log(1.0) - 1.3862944 * jax.random.uniform(keys[2], (TOKENS, TOP), jnp.float32) ** level_of(keys[2], (TOKENS, TOP), ((0, 32),), -0.2, 0.2)), 0.25, 1.0)
    w_gate = scatter_about(keys[3], (EXPERTS, FF, D), D ** -0.5, 0.125, ((0, 8),))
    w_up = scatter_about(keys[4], (EXPERTS, FF, D), D ** -0.5, 0.125, ((0, 8),))
    w_down = scatter_about(keys[5], (EXPERTS, FF, D), FF ** -0.5, 0.21875, ((0, 8),))
    out_grad = scatter_about(keys[6], (TOKENS, D), 1.0, 6.0, ((0, 32),))
    return dict(tokens=tokens, expert_ids=expert_ids, gate_weights=gate_weights, w_gate=w_gate, w_up=w_up, w_down=w_down, out_grad=out_grad)


def silu_grad(value):
    sigmoid_value = jax.nn.sigmoid(value)
    return sigmoid_value * (1.0 + value * (1.0 - sigmoid_value))

def reference(tokens, expert_ids, gate_weights, w_gate, w_up, w_down, out_grad):
    flat_ids = expert_ids.reshape(-1)
    flat_gates = gate_weights.reshape(-1)
    row_limit = CAP * (TOKENS // TOK_DEV)
    out_start = jnp.zeros((TOKENS, D), jnp.float32)
    grad_start = jnp.zeros((TOKENS, D), jnp.float32)
    gate_start = jnp.zeros((TOKENS * TOP,), jnp.float32)

    def one_expert(carry, expert):
        out_acc, grad_acc, gate_acc = carry
        chosen = flat_ids == expert
        where_idx = jnp.nonzero(chosen, size=row_limit, fill_value=0)[0].astype(jnp.int32)
        live_count = jnp.sum(chosen.astype(jnp.int32))
        valid_row = jnp.arange(row_limit, dtype=jnp.int32) < live_count
        token_idx = where_idx // TOP
        picked_rows = jnp.where(valid_row[:, None], tokens[token_idx], jnp.zeros((), tokens.dtype))
        weight = jnp.where(valid_row, flat_gates[where_idx], jnp.zeros((), jnp.float32))
        gate_mat = w_gate[expert]
        up_mat = w_up[expert]
        down_mat = w_down[expert]
        pre_gate = jnp.dot(picked_rows, gate_mat.T, preferred_element_type=jnp.float32)
        pre_up = jnp.dot(picked_rows, up_mat.T, preferred_element_type=jnp.float32)
        activated = jax.nn.silu(pre_gate)
        hidden = (activated * pre_up).astype(jnp.bfloat16)
        expert_out = jnp.dot(hidden, down_mat, preferred_element_type=jnp.float32).astype(jnp.bfloat16)
        out_float = expert_out.astype(jnp.float32)
        out_acc = out_acc.at[token_idx].add(weight[:, None] * out_float)
        grad_rows = out_grad[token_idx].astype(jnp.float32)
        products = lax.optimization_barrier(jnp.sum(grad_rows * out_float, axis=1))
        gate_acc = gate_acc.at[where_idx].add(jnp.where(valid_row, products, jnp.zeros((), jnp.float32)))
        scaled_grad = (weight[:, None] * grad_rows).astype(jnp.bfloat16)
        hidden_grad = jnp.dot(scaled_grad, down_mat.T, preferred_element_type=jnp.float32)
        gate_pre_grad = (hidden_grad * pre_up * silu_grad(pre_gate)).astype(jnp.bfloat16)
        up_pre_grad = (hidden_grad * activated).astype(jnp.bfloat16)
        token_part = (jnp.dot(gate_pre_grad, gate_mat, preferred_element_type=jnp.float32) + jnp.dot(up_pre_grad, up_mat, preferred_element_type=jnp.float32)).astype(jnp.bfloat16)
        grad_acc = grad_acc.at[token_idx].add(token_part.astype(jnp.float32))
        gate_w = jnp.dot(gate_pre_grad.T, picked_rows, preferred_element_type=jnp.float32).astype(jnp.bfloat16)
        up_w = jnp.dot(up_pre_grad.T, picked_rows, preferred_element_type=jnp.float32).astype(jnp.bfloat16)
        down_w = jnp.dot(hidden.T, scaled_grad, preferred_element_type=jnp.float32).astype(jnp.bfloat16)
        return ((out_acc, grad_acc, gate_acc), (gate_w, up_w, down_w))
    carry, stacked = lax.scan(one_expert, (out_start, grad_start, gate_start), jnp.arange(EXPERTS, dtype=jnp.int32))
    out_acc, grad_acc, gate_acc = carry
    gate_w_grad, up_w_grad, down_w_grad = stacked
    layer_out = out_acc.astype(jnp.bfloat16)
    tokens_grad = grad_acc.astype(jnp.bfloat16)
    gates_grad = gate_acc.reshape(TOKENS, TOP)
    return (layer_out, tokens_grad, gates_grad, gate_w_grad, up_w_grad, down_w_grad)
```

```python
import jax
import jax.numpy as jnp
from jax import lax
from jax.sharding import PartitionSpec as P

STRIPE = 16


def silu_grad(value):
    sigmoid_value = jax.nn.sigmoid(value)
    return sigmoid_value * (1.0 + value * (1.0 - sigmoid_value))


def rows_times(left, right):
    return lax.dot_general(
        left, right, (((1,), (1,)), ((), ())), preferred_element_type=jnp.float32
    )


def inner_rows(left, right):
    return lax.dot_general(
        left, right, (((0,), (0,)), ((), ())), preferred_element_type=jnp.float32
    )


def matmul(left, right):
    return jnp.dot(left, right, preferred_element_type=jnp.float32)


def body(tokens, expert_ids, gate_weights, w_gate, w_up, w_down, out_grad):
    tok_count, feature_width = tokens.shape
    top_count = expert_ids.shape[1]
    experts = lax.axis_size("ep")
    per_pair = tok_count // 8
    total_slots = experts * per_pair
    live_cols = min(top_count, -(-experts // STRIPE))
    assigned = tok_count * live_cols

    flat_ids = expert_ids[:, :live_cols].reshape(-1)
    flat_gates = gate_weights[:, :live_cols].reshape(-1)
    live_mask = flat_ids < experts
    onehot = flat_ids[:, None] == jnp.arange(experts, dtype=jnp.int32)[None, :]
    position = jnp.arange(assigned, dtype=jnp.int32)
    earlier = (position[:, None] > position[None, :]).astype(jnp.bfloat16)
    before = matmul(earlier, onehot.astype(jnp.bfloat16))
    slot_rank = jnp.sum(jnp.where(onehot, before, 0.0), axis=1).astype(jnp.int32)
    slot_index = jnp.where(live_mask, flat_ids * per_pair + slot_rank, -1)

    slot_ids = jnp.arange(total_slots, dtype=jnp.int32)
    hit = slot_ids[:, None] == slot_index[None, :]
    slot_gate = jnp.sum(jnp.where(hit, flat_gates[None, :], 0.0), axis=1)
    pick = jnp.any(hit.reshape(total_slots, tok_count, live_cols), axis=2).astype(jnp.bfloat16)
    send_rows = matmul(pick, tokens).astype(jnp.bfloat16)
    grad_rows = matmul(pick, out_grad)
    scaled_grad = (slot_gate[:, None] * grad_rows).astype(jnp.bfloat16)

    outgoing = jnp.concatenate([send_rows, scaled_grad], axis=1)
    received = lax.all_to_all(
        outgoing.reshape(experts, per_pair, 2 * feature_width),
        "ep",
        split_axis=0,
        concat_axis=0,
        tiled=True,
    ).reshape(total_slots, 2 * feature_width)

    gathered = lax.all_gather(received, "rep", axis=0, tiled=True)

    rows_in = received[:, :feature_width]
    grad_in = received[:, feature_width:]
    gate_mat = w_gate[0]
    up_mat = w_up[0]
    down_mat = w_down[0]
    pre_gate = rows_times(rows_in, gate_mat)
    pre_up = rows_times(rows_in, up_mat)
    activated = jax.nn.silu(pre_gate)
    hidden = (activated * pre_up).astype(jnp.bfloat16)
    expert_out = matmul(hidden, down_mat).astype(jnp.bfloat16)
    returned = lax.all_to_all(
        expert_out.reshape(experts, per_pair, feature_width),
        "ep",
        split_axis=0,
        concat_axis=0,
        tiled=True,
    ).reshape(total_slots, feature_width)

    hidden_grad = rows_times(grad_in, down_mat)
    gate_pre_grad = (hidden_grad * pre_up * silu_grad(pre_gate)).astype(jnp.bfloat16)
    up_pre_grad = (hidden_grad * activated).astype(jnp.bfloat16)
    token_part = (
        matmul(gate_pre_grad, gate_mat) + matmul(up_pre_grad, up_mat)
    ).astype(jnp.bfloat16)
    part_back = lax.all_to_all(
        token_part.reshape(experts, per_pair, feature_width),
        "ep",
        split_axis=0,
        concat_axis=0,
        tiled=True,
    ).reshape(total_slots, feature_width)

    slot_grid = slot_index.reshape(tok_count, live_cols)
    gate_grid = flat_gates.reshape(tok_count, live_cols)
    layer_sum = jnp.zeros((tok_count, feature_width), jnp.float32)
    gate_cols = []
    back_pick = jnp.zeros((tok_count, total_slots), jnp.bfloat16)
    for col in range(live_cols):
        col_pick = (slot_grid[:, col : col + 1] == slot_ids[None, :]).astype(jnp.bfloat16)
        back_pick = back_pick + col_pick
        out_rows = matmul(col_pick, returned)
        layer_sum = layer_sum + gate_grid[:, col : col + 1] * out_rows
        gate_cols.append(jnp.sum(out_grad.astype(jnp.float32) * out_rows, axis=1))
    layer_out = layer_sum.astype(jnp.bfloat16)
    gate_cols.extend(
        [jnp.zeros((tok_count,), jnp.float32)] * (top_count - live_cols)
    )
    gates_grad = jnp.stack(gate_cols, axis=1)
    tokens_grad = matmul(back_pick, part_back).astype(jnp.bfloat16)

    share = gate_mat.shape[0] // lax.axis_size("rep")
    start = lax.axis_index("rep") * share
    gate_share = lax.dynamic_slice_in_dim(gate_mat, start, share, axis=0)
    up_share = lax.dynamic_slice_in_dim(up_mat, start, share, axis=0)
    down_share = lax.dynamic_slice_in_dim(down_mat, start, share, axis=0)
    rows_all = gathered[:, :feature_width]
    grad_all = gathered[:, feature_width:]
    pre_gate_s = rows_times(rows_all, gate_share)
    pre_up_s = rows_times(rows_all, up_share)
    activated_s = jax.nn.silu(pre_gate_s)
    hidden_s = (activated_s * pre_up_s).astype(jnp.bfloat16)
    hidden_grad_s = rows_times(grad_all, down_share)
    gate_pre_grad_s = (hidden_grad_s * pre_up_s * silu_grad(pre_gate_s)).astype(jnp.bfloat16)
    up_pre_grad_s = (hidden_grad_s * activated_s).astype(jnp.bfloat16)
    gate_w_grad = inner_rows(gate_pre_grad_s, rows_all).astype(jnp.bfloat16)[None]
    up_w_grad = inner_rows(up_pre_grad_s, rows_all).astype(jnp.bfloat16)[None]
    down_w_grad = inner_rows(hidden_s, grad_all).astype(jnp.bfloat16)[None]
    return (layer_out, tokens_grad, gates_grad, gate_w_grad, up_w_grad, down_w_grad)


def solution(mesh):
    return jax.shard_map(
        body,
        mesh=mesh,
        in_specs=(
            P(("rep", "ep"), None),
            P(("rep", "ep"), None),
            P(("rep", "ep"), None),
            P("ep", None, None),
            P("ep", None, None),
            P("ep", None, None),
            P(("rep", "ep"), None),
        ),
        out_specs=(
            P(("rep", "ep"), None),
            P(("rep", "ep"), None),
            P(("rep", "ep"), None),
            P("ep", "rep", None),
            P("ep", "rep", None),
            P("ep", "rep", None),
        ),
        check_vma=False,
    )
```

```python
import jax
import jax.numpy as jnp
from jax import lax
from jax.sharding import PartitionSpec as P

STRIPE = 16


def silu_grad(value):
    sigmoid_value = jax.nn.sigmoid(value)
    return sigmoid_value * (1.0 + value * (1.0 - sigmoid_value))


def rows_times(left, right):
    return lax.dot_general(
        left, right, (((1,), (1,)), ((), ())), preferred_element_type=jnp.float32
    )


def inner_rows(left, right):
    return lax.dot_general(
        left, right, (((0,), (0,)), ((), ())), preferred_element_type=jnp.float32
    )


def matmul(left, right):
    return jnp.dot(left, right, preferred_element_type=jnp.float32)


def body(tokens, expert_ids, gate_weights, w_gate, w_up, w_down, out_grad):
    tok_count, feature_width = tokens.shape
    top_count = expert_ids.shape[1]
    experts = lax.axis_size("ep")
    per_pair = tok_count // 8
    total_slots = experts * per_pair
    live_cols = min(top_count, -(-experts // STRIPE))
    assigned = tok_count * live_cols

    flat_ids = expert_ids[:, :live_cols].reshape(-1)
    flat_gates = gate_weights[:, :live_cols].reshape(-1)
    live_mask = flat_ids < experts
    onehot = flat_ids[:, None] == jnp.arange(experts, dtype=jnp.int32)[None, :]
    position = jnp.arange(assigned, dtype=jnp.int32)
    earlier = (position[:, None] > position[None, :]).astype(jnp.bfloat16)
    before = matmul(earlier, onehot.astype(jnp.bfloat16))
    slot_rank = jnp.sum(jnp.where(onehot, before, 0.0), axis=1).astype(jnp.int32)
    slot_index = jnp.where(live_mask, flat_ids * per_pair + slot_rank, -1)

    slot_ids = jnp.arange(total_slots, dtype=jnp.int32)
    hit = slot_ids[:, None] == slot_index[None, :]
    slot_gate = jnp.sum(jnp.where(hit, flat_gates[None, :], 0.0), axis=1)
    pick = jnp.any(hit.reshape(total_slots, tok_count, live_cols), axis=2).astype(jnp.bfloat16)
    send_rows = matmul(pick, tokens).astype(jnp.bfloat16)
    grad_rows = matmul(pick, out_grad)
    scaled_grad = (slot_gate[:, None] * grad_rows).astype(jnp.bfloat16)

    def exchange(rows):
        return lax.all_to_all(
            rows.reshape(experts, per_pair, feature_width),
            "ep",
            split_axis=0,
            concat_axis=0,
            tiled=True,
        ).reshape(total_slots, feature_width)

    rows_in = exchange(send_rows)
    rows_all = lax.all_gather(rows_in, "rep", axis=0, tiled=True)
    grad_in = exchange(scaled_grad)
    grad_all = lax.all_gather(grad_in, "rep", axis=0, tiled=True)

    gate_mat = w_gate[0]
    up_mat = w_up[0]
    down_mat = w_down[0]
    pre_gate = rows_times(rows_in, gate_mat)
    pre_up = rows_times(rows_in, up_mat)
    activated = jax.nn.silu(pre_gate)
    hidden = (activated * pre_up).astype(jnp.bfloat16)
    expert_out = matmul(hidden, down_mat).astype(jnp.bfloat16)
    expert_out, rows_all = lax.optimization_barrier((expert_out, rows_all))
    returned = exchange(expert_out)

    hidden_grad = rows_times(grad_in, down_mat)
    gate_pre_grad = (hidden_grad * pre_up * silu_grad(pre_gate)).astype(jnp.bfloat16)
    up_pre_grad = (hidden_grad * activated).astype(jnp.bfloat16)
    token_part = (
        matmul(gate_pre_grad, gate_mat) + matmul(up_pre_grad, up_mat)
    ).astype(jnp.bfloat16)
    token_part, grad_all = lax.optimization_barrier((token_part, grad_all))
    part_back = exchange(token_part)

    slot_grid = slot_index.reshape(tok_count, live_cols)
    gate_grid = flat_gates.reshape(tok_count, live_cols)
    layer_sum = jnp.zeros((tok_count, feature_width), jnp.float32)
    gate_cols = []
    back_pick = jnp.zeros((tok_count, total_slots), jnp.bfloat16)
    for col in range(live_cols):
        col_pick = (slot_grid[:, col : col + 1] == slot_ids[None, :]).astype(jnp.bfloat16)
        back_pick = back_pick + col_pick
        out_rows = matmul(col_pick, returned)
        layer_sum = layer_sum + gate_grid[:, col : col + 1] * out_rows
        gate_cols.append(jnp.sum(out_grad.astype(jnp.float32) * out_rows, axis=1))
    layer_out = layer_sum.astype(jnp.bfloat16)
    gate_cols.extend(
        [jnp.zeros((tok_count,), jnp.float32)] * (top_count - live_cols)
    )
    gates_grad = jnp.stack(gate_cols, axis=1)
    tokens_grad = matmul(back_pick, part_back).astype(jnp.bfloat16)

    share = gate_mat.shape[0] // lax.axis_size("rep")
    start = lax.axis_index("rep") * share
    gate_share = lax.dynamic_slice_in_dim(gate_mat, start, share, axis=0)
    up_share = lax.dynamic_slice_in_dim(up_mat, start, share, axis=0)
    down_share = lax.dynamic_slice_in_dim(down_mat, start, share, axis=0)
    pre_gate_s = rows_times(rows_all, gate_share)
    pre_up_s = rows_times(rows_all, up_share)
    activated_s = jax.nn.silu(pre_gate_s)
    hidden_s = (activated_s * pre_up_s).astype(jnp.bfloat16)
    hidden_grad_s = rows_times(grad_all, down_share)
    gate_pre_grad_s = (hidden_grad_s * pre_up_s * silu_grad(pre_gate_s)).astype(jnp.bfloat16)
    up_pre_grad_s = (hidden_grad_s * activated_s).astype(jnp.bfloat16)
    gate_w_grad = inner_rows(gate_pre_grad_s, rows_all).astype(jnp.bfloat16)[None]
    up_w_grad = inner_rows(up_pre_grad_s, rows_all).astype(jnp.bfloat16)[None]
    down_w_grad = inner_rows(hidden_s, grad_all).astype(jnp.bfloat16)[None]
    return (layer_out, tokens_grad, gates_grad, gate_w_grad, up_w_grad, down_w_grad)


def solution(mesh):
    return jax.shard_map(
        body,
        mesh=mesh,
        in_specs=(
            P(("rep", "ep"), None),
            P(("rep", "ep"), None),
            P(("rep", "ep"), None),
            P("ep", None, None),
            P("ep", None, None),
            P("ep", None, None),
            P(("rep", "ep"), None),
        ),
        out_specs=(
            P(("rep", "ep"), None),
            P(("rep", "ep"), None),
            P(("rep", "ep"), None),
            P("ep", "rep", None),
            P("ep", "rep", None),
            P("ep", "rep", None),
        ),
        check_vma=False,
    )
```

```python
import jax
import jax.numpy as jnp
from jax import lax
from jax.sharding import PartitionSpec as P

STRIPE = 16


def silu_grad(value):
    sigmoid_value = jax.nn.sigmoid(value)
    return sigmoid_value * (1.0 + value * (1.0 - sigmoid_value))


def rows_times(left, right):
    return lax.dot_general(
        left, right, (((1,), (1,)), ((), ())), preferred_element_type=jnp.float32
    )


def inner_rows(left, right):
    return lax.dot_general(
        left, right, (((0,), (0,)), ((), ())), preferred_element_type=jnp.float32
    )


def matmul(left, right):
    return jnp.dot(left, right, preferred_element_type=jnp.float32)


def body(tokens, expert_ids, gate_weights, w_gate, w_up, w_down, out_grad):
    tok_count, feature_width = tokens.shape
    top_count = expert_ids.shape[1]
    experts = lax.axis_size("ep")
    per_pair = tok_count // 8
    total_slots = experts * per_pair
    live_cols = min(top_count, -(-experts // STRIPE))
    assigned = tok_count * live_cols

    flat_ids = expert_ids[:, :live_cols].reshape(-1)
    flat_gates = gate_weights[:, :live_cols].reshape(-1)
    live_mask = flat_ids < experts
    onehot = flat_ids[:, None] == jnp.arange(experts, dtype=jnp.int32)[None, :]
    position = jnp.arange(assigned, dtype=jnp.int32)
    earlier = (position[:, None] > position[None, :]).astype(jnp.bfloat16)
    before = matmul(earlier, onehot.astype(jnp.bfloat16))
    slot_rank = jnp.sum(jnp.where(onehot, before, 0.0), axis=1).astype(jnp.int32)
    slot_index = jnp.where(live_mask, flat_ids * per_pair + slot_rank, -1)

    slot_ids = jnp.arange(total_slots, dtype=jnp.int32)
    hit = slot_ids[:, None] == slot_index[None, :]
    slot_gate = jnp.sum(jnp.where(hit, flat_gates[None, :], 0.0), axis=1)
    pick = jnp.any(hit.reshape(total_slots, tok_count, live_cols), axis=2).astype(jnp.bfloat16)
    send_rows = matmul(pick, tokens).astype(jnp.bfloat16)
    grad_rows = matmul(pick, out_grad)
    scaled_grad = (slot_gate[:, None] * grad_rows).astype(jnp.bfloat16)

    outgoing = jnp.concatenate([send_rows, scaled_grad], axis=1)
    received = lax.all_to_all(
        outgoing.reshape(experts, per_pair, 2 * feature_width),
        "ep",
        split_axis=0,
        concat_axis=0,
        tiled=True,
    ).reshape(total_slots, 2 * feature_width)

    copies = lax.axis_size("rep")
    if copies == 4:
        far = lax.ppermute(received, "rep", [(r, r ^ 2) for r in range(copies)])
    else:
        gathered = lax.all_gather(received, "rep", axis=0, tiled=True)

    rows_in = received[:, :feature_width]
    grad_in = received[:, feature_width:]
    gate_mat = w_gate[0]
    up_mat = w_up[0]
    down_mat = w_down[0]
    pre_gate = rows_times(rows_in, gate_mat)
    pre_up = rows_times(rows_in, up_mat)
    activated = jax.nn.silu(pre_gate)
    hidden = (activated * pre_up).astype(jnp.bfloat16)
    expert_out = matmul(hidden, down_mat).astype(jnp.bfloat16)
    returned = lax.all_to_all(
        expert_out.reshape(experts, per_pair, feature_width),
        "ep",
        split_axis=0,
        concat_axis=0,
        tiled=True,
    ).reshape(total_slots, feature_width)

    hidden_grad = rows_times(grad_in, down_mat)
    gate_pre_grad = (hidden_grad * pre_up * silu_grad(pre_gate)).astype(jnp.bfloat16)
    up_pre_grad = (hidden_grad * activated).astype(jnp.bfloat16)
    token_part = (
        matmul(gate_pre_grad, gate_mat) + matmul(up_pre_grad, up_mat)
    ).astype(jnp.bfloat16)
    if copies == 4:
        token_part, far = lax.optimization_barrier((token_part, far))
        pair = jnp.concatenate([received, far], axis=0)
        near = lax.ppermute(pair, "rep", [(r, r ^ 1) for r in range(copies)])
        gathered = jnp.concatenate([pair, near], axis=0)
    part_back = lax.all_to_all(
        token_part.reshape(experts, per_pair, feature_width),
        "ep",
        split_axis=0,
        concat_axis=0,
        tiled=True,
    ).reshape(total_slots, feature_width)

    slot_grid = slot_index.reshape(tok_count, live_cols)
    gate_grid = flat_gates.reshape(tok_count, live_cols)
    layer_sum = jnp.zeros((tok_count, feature_width), jnp.float32)
    gate_cols = []
    back_pick = jnp.zeros((tok_count, total_slots), jnp.bfloat16)
    for col in range(live_cols):
        col_pick = (slot_grid[:, col : col + 1] == slot_ids[None, :]).astype(jnp.bfloat16)
        back_pick = back_pick + col_pick
        out_rows = matmul(col_pick, returned)
        layer_sum = layer_sum + gate_grid[:, col : col + 1] * out_rows
        gate_cols.append(jnp.sum(out_grad.astype(jnp.float32) * out_rows, axis=1))
    layer_out = layer_sum.astype(jnp.bfloat16)
    gate_cols.extend(
        [jnp.zeros((tok_count,), jnp.float32)] * (top_count - live_cols)
    )
    gates_grad = jnp.stack(gate_cols, axis=1)

    share = gate_mat.shape[0] // lax.axis_size("rep")
    start = lax.axis_index("rep") * share
    gate_share = lax.dynamic_slice_in_dim(gate_mat, start, share, axis=0)
    up_share = lax.dynamic_slice_in_dim(up_mat, start, share, axis=0)
    down_share = lax.dynamic_slice_in_dim(down_mat, start, share, axis=0)
    rows_all = gathered[:, :feature_width]
    grad_all = gathered[:, feature_width:]
    pre_gate_s = rows_times(rows_all, gate_share)
    pre_up_s = rows_times(rows_all, up_share)
    activated_s = jax.nn.silu(pre_gate_s)
    hidden_s = (activated_s * pre_up_s).astype(jnp.bfloat16)
    hidden_grad_s = rows_times(grad_all, down_share)
    gate_pre_grad_s = (hidden_grad_s * pre_up_s * silu_grad(pre_gate_s)).astype(jnp.bfloat16)
    up_pre_grad_s = (hidden_grad_s * activated_s).astype(jnp.bfloat16)
    gate_w_grad = inner_rows(gate_pre_grad_s, rows_all).astype(jnp.bfloat16)[None]
    up_w_grad = inner_rows(up_pre_grad_s, rows_all).astype(jnp.bfloat16)[None]
    down_w_grad = inner_rows(hidden_s, grad_all).astype(jnp.bfloat16)[None]
    part_back, gate_w_grad, up_w_grad, down_w_grad = lax.optimization_barrier(
        (part_back, gate_w_grad, up_w_grad, down_w_grad)
    )
    tokens_grad = matmul(back_pick, part_back).astype(jnp.bfloat16)
    return (layer_out, tokens_grad, gates_grad, gate_w_grad, up_w_grad, down_w_grad)


def solution(mesh):
    return jax.shard_map(
        body,
        mesh=mesh,
        in_specs=(
            P(("rep", "ep"), None),
            P(("rep", "ep"), None),
            P(("rep", "ep"), None),
            P("ep", None, None),
            P("ep", None, None),
            P("ep", None, None),
            P(("rep", "ep"), None),
        ),
        out_specs=(
            P(("rep", "ep"), None),
            P(("rep", "ep"), None),
            P(("rep", "ep"), None),
            P("ep", "rep", None),
            P("ep", "rep", None),
            P("ep", "rep", None),
        ),
        check_vma=False,
    )
```

```python
import jax
import jax.numpy as jnp
from jax import lax
from jax.sharding import PartitionSpec as P

STRIPE = 16


def silu_grad(value):
    sigmoid_value = jax.nn.sigmoid(value)
    return sigmoid_value * (1.0 + value * (1.0 - sigmoid_value))


def rows_times(left, right):
    return lax.dot_general(
        left, right, (((1,), (1,)), ((), ())), preferred_element_type=jnp.float32
    )


def inner_rows(left, right):
    return lax.dot_general(
        left, right, (((0,), (0,)), ((), ())), preferred_element_type=jnp.float32
    )


def matmul(left, right):
    return jnp.dot(left, right, preferred_element_type=jnp.float32)


def body(tokens, expert_ids, gate_weights, w_gate, w_up, w_down, out_grad):
    tok_count, feature_width = tokens.shape
    top_count = expert_ids.shape[1]
    experts = lax.axis_size("ep")
    per_pair = tok_count // 8
    total_slots = experts * per_pair
    live_cols = min(top_count, -(-experts // STRIPE))
    assigned = tok_count * live_cols

    flat_ids = expert_ids[:, :live_cols].reshape(-1)
    flat_gates = gate_weights[:, :live_cols].reshape(-1)
    live_mask = flat_ids < experts
    onehot = flat_ids[:, None] == jnp.arange(experts, dtype=jnp.int32)[None, :]
    position = jnp.arange(assigned, dtype=jnp.int32)
    earlier = (position[:, None] > position[None, :]).astype(jnp.bfloat16)
    before = matmul(earlier, onehot.astype(jnp.bfloat16))
    slot_rank = jnp.sum(jnp.where(onehot, before, 0.0), axis=1).astype(jnp.int32)
    slot_index = jnp.where(live_mask, flat_ids * per_pair + slot_rank, -1)

    slot_ids = jnp.arange(total_slots, dtype=jnp.int32)
    hit = slot_ids[:, None] == slot_index[None, :]
    slot_gate = jnp.sum(jnp.where(hit, flat_gates[None, :], 0.0), axis=1)
    pick = jnp.any(hit.reshape(total_slots, tok_count, live_cols), axis=2).astype(jnp.bfloat16)
    send_rows = matmul(pick, tokens).astype(jnp.bfloat16)
    grad_rows = matmul(pick, out_grad)
    scaled_grad = (slot_gate[:, None] * grad_rows).astype(jnp.bfloat16)

    outgoing = jnp.concatenate([send_rows, scaled_grad], axis=1)
    received = lax.all_to_all(
        outgoing.reshape(experts, per_pair, 2 * feature_width),
        "ep",
        split_axis=0,
        concat_axis=0,
        tiled=True,
    ).reshape(total_slots, 2 * feature_width)

    gathered = lax.all_gather(received, "rep", axis=0, tiled=True)

    rows_in = received[:, :feature_width]
    grad_in = received[:, feature_width:]
    gate_mat = w_gate[0]
    up_mat = w_up[0]
    down_mat = w_down[0]
    pre_gate = rows_times(rows_in, gate_mat)
    pre_up = rows_times(rows_in, up_mat)
    activated = jax.nn.silu(pre_gate)
    hidden = (activated * pre_up).astype(jnp.bfloat16)
    expert_out = matmul(hidden, down_mat).astype(jnp.bfloat16)
    returned = lax.all_to_all(
        expert_out.reshape(experts, per_pair, feature_width),
        "ep",
        split_axis=0,
        concat_axis=0,
        tiled=True,
    ).reshape(total_slots, feature_width)

    hidden_grad = rows_times(grad_in, down_mat)
    gate_pre_grad = (hidden_grad * pre_up * silu_grad(pre_gate)).astype(jnp.bfloat16)
    up_pre_grad = (hidden_grad * activated).astype(jnp.bfloat16)
    token_part = (
        matmul(gate_pre_grad, gate_mat) + matmul(up_pre_grad, up_mat)
    ).astype(jnp.bfloat16)
    part_back = lax.all_to_all(
        token_part.reshape(experts, per_pair, feature_width),
        "ep",
        split_axis=0,
        concat_axis=0,
        tiled=True,
    ).reshape(total_slots, feature_width)

    slot_grid = slot_index.reshape(tok_count, live_cols)
    gate_grid = flat_gates.reshape(tok_count, live_cols)
    layer_sum = jnp.zeros((tok_count, feature_width), jnp.float32)
    gate_cols = []
    back_pick = jnp.zeros((tok_count, total_slots), jnp.bfloat16)
    for col in range(live_cols):
        col_pick = (slot_grid[:, col : col + 1] == slot_ids[None, :]).astype(jnp.bfloat16)
        back_pick = back_pick + col_pick
        out_rows = matmul(col_pick, returned)
        layer_sum = layer_sum + gate_grid[:, col : col + 1] * out_rows
        gate_cols.append(jnp.sum(out_grad.astype(jnp.float32) * out_rows, axis=1))
    layer_out = layer_sum.astype(jnp.bfloat16)
    gate_cols.extend(
        [jnp.zeros((tok_count,), jnp.float32)] * (top_count - live_cols)
    )
    gates_grad = jnp.stack(gate_cols, axis=1)

    share = gate_mat.shape[0] // lax.axis_size("rep")
    start = lax.axis_index("rep") * share
    gate_share = lax.dynamic_slice_in_dim(gate_mat, start, share, axis=0)
    up_share = lax.dynamic_slice_in_dim(up_mat, start, share, axis=0)
    down_share = lax.dynamic_slice_in_dim(down_mat, start, share, axis=0)
    rows_all = gathered[:, :feature_width]
    grad_all = gathered[:, feature_width:]
    pre_gate_s = rows_times(rows_all, gate_share)
    pre_up_s = rows_times(rows_all, up_share)
    activated_s = jax.nn.silu(pre_gate_s)
    hidden_s = (activated_s * pre_up_s).astype(jnp.bfloat16)
    hidden_grad_s = rows_times(grad_all, down_share)
    gate_pre_grad_s = (hidden_grad_s * pre_up_s * silu_grad(pre_gate_s)).astype(jnp.bfloat16)
    up_pre_grad_s = (hidden_grad_s * activated_s).astype(jnp.bfloat16)
    gate_w_grad = inner_rows(gate_pre_grad_s, rows_all).astype(jnp.bfloat16)[None]
    up_w_grad = inner_rows(up_pre_grad_s, rows_all).astype(jnp.bfloat16)[None]
    down_w_grad = inner_rows(hidden_s, grad_all).astype(jnp.bfloat16)[None]
    part_back, gate_w_grad, up_w_grad, down_w_grad = lax.optimization_barrier(
        (part_back, gate_w_grad, up_w_grad, down_w_grad)
    )
    tokens_grad = matmul(back_pick, part_back).astype(jnp.bfloat16)
    return (layer_out, tokens_grad, gates_grad, gate_w_grad, up_w_grad, down_w_grad)


def solution(mesh):
    return jax.shard_map(
        body,
        mesh=mesh,
        in_specs=(
            P(("rep", "ep"), None),
            P(("rep", "ep"), None),
            P(("rep", "ep"), None),
            P("ep", None, None),
            P("ep", None, None),
            P("ep", None, None),
            P(("rep", "ep"), None),
        ),
        out_specs=(
            P(("rep", "ep"), None),
            P(("rep", "ep"), None),
            P(("rep", "ep"), None),
            P("ep", "rep", None),
            P("ep", "rep", None),
            P("ep", "rep", None),
        ),
        check_vma=False,
    )
```

```python
import jax
import jax.numpy as jnp
from jax import lax
from jax.sharding import PartitionSpec as P

STRIPE = 16


def silu_grad(value):
    sigmoid_value = jax.nn.sigmoid(value)
    return sigmoid_value * (1.0 + value * (1.0 - sigmoid_value))


def rows_times(left, right):
    return lax.dot_general(
        left, right, (((1,), (1,)), ((), ())), preferred_element_type=jnp.float32
    )


def inner_rows(left, right):
    return lax.dot_general(
        left, right, (((0,), (0,)), ((), ())), preferred_element_type=jnp.float32
    )


def matmul(left, right):
    return jnp.dot(left, right, preferred_element_type=jnp.float32)


def body(tokens, expert_ids, gate_weights, w_gate, w_up, w_down, out_grad):
    tok_count, feature_width = tokens.shape
    top_count = expert_ids.shape[1]
    experts = lax.axis_size("ep")
    per_pair = tok_count // 8
    total_slots = experts * per_pair
    live_cols = min(top_count, -(-experts // STRIPE))
    assigned = tok_count * live_cols

    flat_ids = expert_ids[:, :live_cols].reshape(-1)
    flat_gates = gate_weights[:, :live_cols].reshape(-1)
    live_mask = flat_ids < experts
    onehot = flat_ids[:, None] == jnp.arange(experts, dtype=jnp.int32)[None, :]
    position = jnp.arange(assigned, dtype=jnp.int32)
    earlier = (position[:, None] > position[None, :]).astype(jnp.bfloat16)
    before = matmul(earlier, onehot.astype(jnp.bfloat16))
    slot_rank = jnp.sum(jnp.where(onehot, before, 0.0), axis=1).astype(jnp.int32)
    slot_index = jnp.where(live_mask, flat_ids * per_pair + slot_rank, -1)

    slot_ids = jnp.arange(total_slots, dtype=jnp.int32)
    hit = slot_ids[:, None] == slot_index[None, :]
    slot_gate = jnp.sum(jnp.where(hit, flat_gates[None, :], 0.0), axis=1)
    pick = jnp.any(hit.reshape(total_slots, tok_count, live_cols), axis=2).astype(jnp.bfloat16)
    send_rows = matmul(pick, tokens).astype(jnp.bfloat16)
    grad_rows = matmul(pick, out_grad)
    scaled_grad = (slot_gate[:, None] * grad_rows).astype(jnp.bfloat16)

    outgoing = jnp.concatenate([send_rows, scaled_grad], axis=1)
    received = lax.all_to_all(
        outgoing.reshape(experts, per_pair, 2 * feature_width),
        "ep",
        split_axis=0,
        concat_axis=0,
        tiled=True,
    ).reshape(total_slots, 2 * feature_width)

    gathered = lax.all_gather(received, "rep", axis=0, tiled=True)

    rows_in = received[:, :feature_width]
    grad_in = received[:, feature_width:]
    gate_mat = w_gate[0]
    up_mat = w_up[0]
    down_mat = w_down[0]
    pre_gate = rows_times(rows_in, gate_mat)
    pre_up = rows_times(rows_in, up_mat)
    activated = jax.nn.silu(pre_gate)
    hidden = (activated * pre_up).astype(jnp.bfloat16)
    expert_out = matmul(hidden, down_mat).astype(jnp.bfloat16)
    returned = lax.all_to_all(
        expert_out.reshape(experts, per_pair, feature_width),
        "ep",
        split_axis=0,
        concat_axis=0,
        tiled=True,
    ).reshape(total_slots, feature_width)

    hidden_grad = rows_times(grad_in, down_mat)
    gate_pre_grad = (hidden_grad * pre_up * silu_grad(pre_gate)).astype(jnp.bfloat16)
    up_pre_grad = (hidden_grad * activated).astype(jnp.bfloat16)
    token_part = (
        matmul(gate_pre_grad, gate_mat) + matmul(up_pre_grad, up_mat)
    ).astype(jnp.bfloat16)
    part_back = lax.all_to_all(
        token_part.reshape(experts, per_pair, feature_width),
        "ep",
        split_axis=0,
        concat_axis=0,
        tiled=True,
    ).reshape(total_slots, feature_width)

    slot_grid = slot_index.reshape(tok_count, live_cols)
    gate_grid = flat_gates.reshape(tok_count, live_cols)
    layer_sum = jnp.zeros((tok_count, feature_width), jnp.float32)
    gate_cols = []
    back_pick = jnp.zeros((tok_count, total_slots), jnp.bfloat16)
    for col in range(live_cols):
        col_pick = (slot_grid[:, col : col + 1] == slot_ids[None, :]).astype(jnp.bfloat16)
        back_pick = back_pick + col_pick
        out_rows = matmul(col_pick, returned)
        layer_sum = layer_sum + gate_grid[:, col : col + 1] * out_rows
        gate_cols.append(jnp.sum(out_grad.astype(jnp.float32) * out_rows, axis=1))
    layer_out = layer_sum.astype(jnp.bfloat16)
    gate_cols.extend(
        [jnp.zeros((tok_count,), jnp.float32)] * (top_count - live_cols)
    )
    gates_grad = jnp.stack(gate_cols, axis=1)

    share = gate_mat.shape[0] // lax.axis_size("rep")
    start = lax.axis_index("rep") * share
    gate_share = lax.dynamic_slice_in_dim(gate_mat, start, share, axis=0)
    up_share = lax.dynamic_slice_in_dim(up_mat, start, share, axis=0)
    down_share = lax.dynamic_slice_in_dim(down_mat, start, share, axis=0)
    rows_all = gathered[:, :feature_width]
    grad_all = gathered[:, feature_width:]
    pre_both = rows_times(rows_all, jnp.concatenate([gate_share, up_share], axis=0))
    pre_gate_s = pre_both[:, :share]
    pre_up_s = pre_both[:, share:]
    activated_s = jax.nn.silu(pre_gate_s)
    hidden_s = (activated_s * pre_up_s).astype(jnp.bfloat16)
    hidden_grad_s = rows_times(grad_all, down_share)
    gate_pre_grad_s = (hidden_grad_s * pre_up_s * silu_grad(pre_gate_s)).astype(jnp.bfloat16)
    up_pre_grad_s = (hidden_grad_s * activated_s).astype(jnp.bfloat16)
    both_w_grad = inner_rows(
        jnp.concatenate([gate_pre_grad_s, up_pre_grad_s], axis=1), rows_all
    ).astype(jnp.bfloat16)
    gate_w_grad = both_w_grad[:share][None]
    up_w_grad = both_w_grad[share:][None]
    down_w_grad = inner_rows(hidden_s, grad_all).astype(jnp.bfloat16)[None]
    part_back, gate_w_grad, up_w_grad, down_w_grad = lax.optimization_barrier(
        (part_back, gate_w_grad, up_w_grad, down_w_grad)
    )
    tokens_grad = matmul(back_pick, part_back).astype(jnp.bfloat16)
    return (layer_out, tokens_grad, gates_grad, gate_w_grad, up_w_grad, down_w_grad)


def solution(mesh):
    return jax.shard_map(
        body,
        mesh=mesh,
        in_specs=(
            P(("rep", "ep"), None),
            P(("rep", "ep"), None),
            P(("rep", "ep"), None),
            P("ep", None, None),
            P("ep", None, None),
            P("ep", None, None),
            P(("rep", "ep"), None),
        ),
        out_specs=(
            P(("rep", "ep"), None),
            P(("rep", "ep"), None),
            P(("rep", "ep"), None),
            P("ep", "rep", None),
            P("ep", "rep", None),
            P("ep", "rep", None),
        ),
        check_vma=False,
    )
```

```python
import jax
import jax.numpy as jnp
from jax import lax
from jax.sharding import PartitionSpec as P

STRIPE = 16


def silu_grad(value):
    sigmoid_value = jax.nn.sigmoid(value)
    return sigmoid_value * (1.0 + value * (1.0 - sigmoid_value))


def rows_times(left, right):
    return lax.dot_general(
        left, right, (((1,), (1,)), ((), ())), preferred_element_type=jnp.float32
    )


def inner_rows(left, right):
    return lax.dot_general(
        left, right, (((0,), (0,)), ((), ())), preferred_element_type=jnp.float32
    )


def matmul(left, right):
    return jnp.dot(left, right, preferred_element_type=jnp.float32)


def body(tokens, expert_ids, gate_weights, w_gate, w_up, w_down, out_grad):
    tok_count, feature_width = tokens.shape
    top_count = expert_ids.shape[1]
    experts = lax.axis_size("ep")
    per_pair = tok_count // 8
    total_slots = experts * per_pair
    live_cols = min(top_count, -(-experts // STRIPE))
    assigned = tok_count * live_cols

    flat_ids = expert_ids[:, :live_cols].reshape(-1)
    flat_gates = gate_weights[:, :live_cols].reshape(-1)
    live_mask = flat_ids < experts
    onehot = flat_ids[:, None] == jnp.arange(experts, dtype=jnp.int32)[None, :]
    position = jnp.arange(assigned, dtype=jnp.int32)
    earlier = (position[:, None] > position[None, :]).astype(jnp.bfloat16)
    before = matmul(earlier, onehot.astype(jnp.bfloat16))
    slot_rank = jnp.sum(jnp.where(onehot, before, 0.0), axis=1).astype(jnp.int32)
    slot_index = jnp.where(live_mask, flat_ids * per_pair + slot_rank, -1)

    slot_ids = jnp.arange(total_slots, dtype=jnp.int32)
    hit = slot_ids[:, None] == slot_index[None, :]
    slot_gate = jnp.sum(jnp.where(hit, flat_gates[None, :], 0.0), axis=1)
    pick = jnp.any(hit.reshape(total_slots, tok_count, live_cols), axis=2).astype(jnp.bfloat16)
    pick = lax.optimization_barrier(pick)
    send_rows = matmul(pick, tokens).astype(jnp.bfloat16)
    grad_rows = matmul(pick, out_grad)
    scaled_grad = (slot_gate[:, None] * grad_rows).astype(jnp.bfloat16)

    outgoing = jnp.concatenate([send_rows, scaled_grad], axis=1)
    received = lax.all_to_all(
        outgoing.reshape(experts, per_pair, 2 * feature_width),
        "ep",
        split_axis=0,
        concat_axis=0,
        tiled=True,
    ).reshape(total_slots, 2 * feature_width)

    gathered = lax.all_gather(received, "rep", axis=0, tiled=True)

    rows_in = received[:, :feature_width]
    grad_in = received[:, feature_width:]
    gate_mat = w_gate[0]
    up_mat = w_up[0]
    down_mat = w_down[0]
    pre_gate = rows_times(rows_in, gate_mat)
    pre_up = rows_times(rows_in, up_mat)
    activated = jax.nn.silu(pre_gate)
    hidden = (activated * pre_up).astype(jnp.bfloat16)
    expert_out = matmul(hidden, down_mat).astype(jnp.bfloat16)
    returned = lax.all_to_all(
        expert_out.reshape(experts, per_pair, feature_width),
        "ep",
        split_axis=0,
        concat_axis=0,
        tiled=True,
    ).reshape(total_slots, feature_width)

    hidden_grad = rows_times(grad_in, down_mat)
    gate_pre_grad = (hidden_grad * pre_up * silu_grad(pre_gate)).astype(jnp.bfloat16)
    up_pre_grad = (hidden_grad * activated).astype(jnp.bfloat16)
    token_part = (
        matmul(gate_pre_grad, gate_mat) + matmul(up_pre_grad, up_mat)
    ).astype(jnp.bfloat16)
    part_back = lax.all_to_all(
        token_part.reshape(experts, per_pair, feature_width),
        "ep",
        split_axis=0,
        concat_axis=0,
        tiled=True,
    ).reshape(total_slots, feature_width)

    slot_grid = slot_index.reshape(tok_count, live_cols)
    gate_grid = flat_gates.reshape(tok_count, live_cols)
    layer_sum = jnp.zeros((tok_count, feature_width), jnp.float32)
    gate_cols = []
    back_pick = jnp.zeros((tok_count, total_slots), jnp.bfloat16)
    for col in range(live_cols):
        col_pick = (slot_grid[:, col : col + 1] == slot_ids[None, :]).astype(jnp.bfloat16)
        back_pick = back_pick + col_pick
        out_rows = matmul(col_pick, returned)
        layer_sum = layer_sum + gate_grid[:, col : col + 1] * out_rows
        gate_cols.append(jnp.sum(out_grad.astype(jnp.float32) * out_rows, axis=1))
    layer_out = layer_sum.astype(jnp.bfloat16)
    back_pick = lax.optimization_barrier(back_pick)
    gate_cols.extend(
        [jnp.zeros((tok_count,), jnp.float32)] * (top_count - live_cols)
    )
    gates_grad = jnp.stack(gate_cols, axis=1)

    share = gate_mat.shape[0] // lax.axis_size("rep")
    start = lax.axis_index("rep") * share
    gate_share = lax.dynamic_slice_in_dim(gate_mat, start, share, axis=0)
    up_share = lax.dynamic_slice_in_dim(up_mat, start, share, axis=0)
    down_share = lax.dynamic_slice_in_dim(down_mat, start, share, axis=0)
    rows_all = gathered[:, :feature_width]
    grad_all = gathered[:, feature_width:]
    pre_both = rows_times(rows_all, jnp.concatenate([gate_share, up_share], axis=0))
    pre_gate_s = pre_both[:, :share]
    pre_up_s = pre_both[:, share:]
    activated_s = jax.nn.silu(pre_gate_s)
    hidden_s = (activated_s * pre_up_s).astype(jnp.bfloat16)
    hidden_grad_s = rows_times(grad_all, down_share)
    gate_pre_grad_s = (hidden_grad_s * pre_up_s * silu_grad(pre_gate_s)).astype(jnp.bfloat16)
    up_pre_grad_s = (hidden_grad_s * activated_s).astype(jnp.bfloat16)
    both_w_grad = inner_rows(
        jnp.concatenate([gate_pre_grad_s, up_pre_grad_s], axis=1), rows_all
    ).astype(jnp.bfloat16)
    gate_w_grad = both_w_grad[:share][None]
    up_w_grad = both_w_grad[share:][None]
    down_w_grad = inner_rows(hidden_s, grad_all).astype(jnp.bfloat16)[None]
    part_back, gate_w_grad, up_w_grad, down_w_grad = lax.optimization_barrier(
        (part_back, gate_w_grad, up_w_grad, down_w_grad)
    )
    tokens_grad = matmul(back_pick, part_back).astype(jnp.bfloat16)
    return (layer_out, tokens_grad, gates_grad, gate_w_grad, up_w_grad, down_w_grad)


def solution(mesh):
    return jax.shard_map(
        body,
        mesh=mesh,
        in_specs=(
            P(("rep", "ep"), None),
            P(("rep", "ep"), None),
            P(("rep", "ep"), None),
            P("ep", None, None),
            P("ep", None, None),
            P("ep", None, None),
            P(("rep", "ep"), None),
        ),
        out_specs=(
            P(("rep", "ep"), None),
            P(("rep", "ep"), None),
            P(("rep", "ep"), None),
            P("ep", "rep", None),
            P("ep", "rep", None),
            P("ep", "rep", None),
        ),
        check_vma=False,
    )
```

```python
import jax
import jax.numpy as jnp
from jax import lax
from jax.sharding import PartitionSpec as P

STRIPE = 16


def silu_grad(value):
    sigmoid_value = jax.nn.sigmoid(value)
    return sigmoid_value * (1.0 + value * (1.0 - sigmoid_value))


def rows_times(left, right):
    return lax.dot_general(
        left, right, (((1,), (1,)), ((), ())), preferred_element_type=jnp.float32
    )


def inner_rows(left, right):
    return lax.dot_general(
        left, right, (((0,), (0,)), ((), ())), preferred_element_type=jnp.float32
    )


def matmul(left, right):
    return jnp.dot(left, right, preferred_element_type=jnp.float32)


def body(tokens, expert_ids, gate_weights, w_gate, w_up, w_down, out_grad):
    tok_count, feature_width = tokens.shape
    top_count = expert_ids.shape[1]
    experts = lax.axis_size("ep")
    per_pair = tok_count // 8
    total_slots = experts * per_pair
    live_cols = min(top_count, -(-experts // STRIPE))
    assigned = tok_count * live_cols

    flat_ids = expert_ids[:, :live_cols].reshape(-1)
    flat_gates = gate_weights[:, :live_cols].reshape(-1)
    live_mask = flat_ids < experts
    onehot = flat_ids[:, None] == jnp.arange(experts, dtype=jnp.int32)[None, :]
    position = jnp.arange(assigned, dtype=jnp.int32)
    earlier = (position[:, None] > position[None, :]).astype(jnp.bfloat16)
    before = matmul(earlier, onehot.astype(jnp.bfloat16))
    slot_rank = jnp.sum(jnp.where(onehot, before, 0.0), axis=1).astype(jnp.int32)
    slot_index = jnp.where(live_mask, flat_ids * per_pair + slot_rank, -1)

    slot_ids = jnp.arange(total_slots, dtype=jnp.int32)
    hit = slot_ids[:, None] == slot_index[None, :]
    slot_gate = jnp.sum(jnp.where(hit, flat_gates[None, :], 0.0), axis=1)
    pick = jnp.any(hit.reshape(total_slots, tok_count, live_cols), axis=2).astype(jnp.bfloat16)
    send_rows = matmul(pick, tokens).astype(jnp.bfloat16)
    grad_rows = matmul(pick, out_grad)
    scaled_grad = (slot_gate[:, None] * grad_rows).astype(jnp.bfloat16)

    outgoing = jnp.concatenate([send_rows, scaled_grad], axis=1)
    received = lax.all_to_all(
        outgoing.reshape(experts, per_pair, 2 * feature_width),
        "ep",
        split_axis=0,
        concat_axis=0,
        tiled=True,
    ).reshape(total_slots, 2 * feature_width)

    gathered = lax.all_gather(received, "rep", axis=0, tiled=True)

    rows_in = received[:, :feature_width]
    grad_in = received[:, feature_width:]
    gate_mat = w_gate[0]
    up_mat = w_up[0]
    down_mat = w_down[0]
    pre_gate = rows_times(rows_in, gate_mat)
    pre_up = rows_times(rows_in, up_mat)
    activated = jax.nn.silu(pre_gate)
    hidden = (activated * pre_up).astype(jnp.bfloat16)
    expert_out = matmul(hidden, down_mat).astype(jnp.bfloat16)
    expert_out, grad_in = lax.optimization_barrier((expert_out, grad_in))
    returned = lax.all_to_all(
        expert_out.reshape(experts, per_pair, feature_width),
        "ep",
        split_axis=0,
        concat_axis=0,
        tiled=True,
    ).reshape(total_slots, feature_width)

    hidden_grad = rows_times(grad_in, down_mat)
    gate_pre_grad = (hidden_grad * pre_up * silu_grad(pre_gate)).astype(jnp.bfloat16)
    up_pre_grad = (hidden_grad * activated).astype(jnp.bfloat16)
    token_part = (
        matmul(gate_pre_grad, gate_mat) + matmul(up_pre_grad, up_mat)
    ).astype(jnp.bfloat16)
    part_back = lax.all_to_all(
        token_part.reshape(experts, per_pair, feature_width),
        "ep",
        split_axis=0,
        concat_axis=0,
        tiled=True,
    ).reshape(total_slots, feature_width)

    slot_grid = slot_index.reshape(tok_count, live_cols)
    gate_grid = flat_gates.reshape(tok_count, live_cols)
    layer_sum = jnp.zeros((tok_count, feature_width), jnp.float32)
    gate_cols = []
    back_pick = jnp.zeros((tok_count, total_slots), jnp.bfloat16)
    for col in range(live_cols):
        col_pick = (slot_grid[:, col : col + 1] == slot_ids[None, :]).astype(jnp.bfloat16)
        back_pick = back_pick + col_pick
        out_rows = matmul(col_pick, returned)
        layer_sum = layer_sum + gate_grid[:, col : col + 1] * out_rows
        gate_cols.append(jnp.sum(out_grad.astype(jnp.float32) * out_rows, axis=1))
    layer_out = layer_sum.astype(jnp.bfloat16)
    gate_cols.extend(
        [jnp.zeros((tok_count,), jnp.float32)] * (top_count - live_cols)
    )
    gates_grad = jnp.stack(gate_cols, axis=1)

    copies = lax.axis_size("rep")
    share = gate_mat.shape[0] // copies

    def by_share(values):
        return values.reshape(total_slots, copies, share).transpose(1, 0, 2)

    own_terms = jnp.concatenate(
        [by_share(gate_pre_grad), by_share(up_pre_grad), by_share(hidden)], axis=2
    )
    me = lax.axis_index("rep")
    blocks = [own_terms[me]] + [
        lax.ppermute(own_terms[me ^ k], "rep", [(r, r ^ k) for r in range(copies)])
        for k in range(1, copies)
    ]
    order = jnp.arange(copies, dtype=jnp.int32) ^ me.astype(jnp.int32)
    terms = jnp.take(jnp.stack(blocks), order, axis=0).reshape(copies * total_slots, 3 * share)
    rows_all = gathered[:, :feature_width]
    grad_all = gathered[:, feature_width:]
    both_w_grad = inner_rows(terms[:, : 2 * share], rows_all).astype(jnp.bfloat16)
    gate_w_grad = both_w_grad[:share][None]
    up_w_grad = both_w_grad[share:][None]
    down_w_grad = inner_rows(terms[:, 2 * share :], grad_all).astype(jnp.bfloat16)[None]
    part_back, gate_w_grad, up_w_grad, down_w_grad = lax.optimization_barrier(
        (part_back, gate_w_grad, up_w_grad, down_w_grad)
    )
    tokens_grad = matmul(back_pick, part_back).astype(jnp.bfloat16)
    return (layer_out, tokens_grad, gates_grad, gate_w_grad, up_w_grad, down_w_grad)


def solution(mesh):
    return jax.shard_map(
        body,
        mesh=mesh,
        in_specs=(
            P(("rep", "ep"), None),
            P(("rep", "ep"), None),
            P(("rep", "ep"), None),
            P("ep", None, None),
            P("ep", None, None),
            P("ep", None, None),
            P(("rep", "ep"), None),
        ),
        out_specs=(
            P(("rep", "ep"), None),
            P(("rep", "ep"), None),
            P(("rep", "ep"), None),
            P("ep", "rep", None),
            P("ep", "rep", None),
            P("ep", "rep", None),
        ),
        check_vma=False,
    )
```

```python
import jax
import jax.numpy as jnp
from jax import lax
from jax.sharding import PartitionSpec as P

STRIPE = 16


def silu_grad(value):
    sigmoid_value = jax.nn.sigmoid(value)
    return sigmoid_value * (1.0 + value * (1.0 - sigmoid_value))


def rows_times(left, right):
    return lax.dot_general(
        left, right, (((1,), (1,)), ((), ())), preferred_element_type=jnp.float32
    )


def inner_rows(left, right):
    return lax.dot_general(
        left, right, (((0,), (0,)), ((), ())), preferred_element_type=jnp.float32
    )


def matmul(left, right):
    return jnp.dot(left, right, preferred_element_type=jnp.float32)


def body(tokens, expert_ids, gate_weights, w_gate, w_up, w_down, out_grad):
    tok_count, feature_width = tokens.shape
    top_count = expert_ids.shape[1]
    experts = lax.axis_size("ep")
    per_pair = tok_count // 8
    total_slots = experts * per_pair
    live_cols = min(top_count, -(-experts // STRIPE))
    assigned = tok_count * live_cols

    column_pick = (
        jnp.arange(top_count, dtype=jnp.int32)[None, :, None]
        == jnp.arange(live_cols, dtype=jnp.int32)[None, None, :]
    )
    flat_ids = jnp.sum(
        jnp.where(column_pick, expert_ids[:, :, None], 0), axis=1
    ).reshape(-1)
    flat_gates = jnp.sum(
        jnp.where(column_pick, gate_weights[:, :, None], 0.0), axis=1
    ).reshape(-1)
    live_mask = flat_ids < experts
    onehot = flat_ids[:, None] == jnp.arange(experts, dtype=jnp.int32)[None, :]
    position = jnp.arange(assigned, dtype=jnp.int32)
    earlier = (position[:, None] > position[None, :]).astype(jnp.bfloat16)
    before = matmul(earlier, onehot.astype(jnp.bfloat16))
    slot_rank = jnp.sum(jnp.where(onehot, before, 0.0), axis=1).astype(jnp.int32)
    slot_index = jnp.where(live_mask, flat_ids * per_pair + slot_rank, -1)

    slot_ids = jnp.arange(total_slots, dtype=jnp.int32)
    hit = slot_ids[:, None] == slot_index[None, :]
    slot_gate = jnp.sum(jnp.where(hit, flat_gates[None, :], 0.0), axis=1)
    pick = jnp.any(hit.reshape(total_slots, tok_count, live_cols), axis=2).astype(jnp.bfloat16)
    send_rows = matmul(pick, tokens).astype(jnp.bfloat16)
    grad_rows = matmul(pick, out_grad)
    scaled_grad = (slot_gate[:, None] * grad_rows).astype(jnp.bfloat16)

    outgoing = jnp.concatenate([send_rows, scaled_grad], axis=1)
    received = lax.all_to_all(
        outgoing.reshape(experts, per_pair, 2 * feature_width),
        "ep",
        split_axis=0,
        concat_axis=0,
        tiled=True,
    ).reshape(total_slots, 2 * feature_width)

    gathered = lax.all_gather(received, "rep", axis=0, tiled=True)

    rows_in = received[:, :feature_width]
    grad_in = received[:, feature_width:]
    gate_mat = w_gate[0]
    up_mat = w_up[0]
    down_mat = w_down[0]
    pre_gate = rows_times(rows_in, gate_mat)
    pre_up = rows_times(rows_in, up_mat)
    activated = jax.nn.silu(pre_gate)
    hidden = (activated * pre_up).astype(jnp.bfloat16)
    expert_out = matmul(hidden, down_mat).astype(jnp.bfloat16)
    returned = lax.all_to_all(
        expert_out.reshape(experts, per_pair, feature_width),
        "ep",
        split_axis=0,
        concat_axis=0,
        tiled=True,
    ).reshape(total_slots, feature_width)

    hidden_grad = rows_times(grad_in, down_mat)
    gate_pre_grad = (hidden_grad * pre_up * silu_grad(pre_gate)).astype(jnp.bfloat16)
    up_pre_grad = (hidden_grad * activated).astype(jnp.bfloat16)
    token_part = (
        matmul(gate_pre_grad, gate_mat) + matmul(up_pre_grad, up_mat)
    ).astype(jnp.bfloat16)
    part_back = lax.all_to_all(
        token_part.reshape(experts, per_pair, feature_width),
        "ep",
        split_axis=0,
        concat_axis=0,
        tiled=True,
    ).reshape(total_slots, feature_width)

    slot_grid = slot_index.reshape(tok_count, live_cols)
    gate_grid = flat_gates.reshape(tok_count, live_cols)
    layer_sum = jnp.zeros((tok_count, feature_width), jnp.float32)
    gate_cols = []
    back_pick = jnp.zeros((tok_count, total_slots), jnp.bfloat16)
    for col in range(live_cols):
        col_pick = (slot_grid[:, col : col + 1] == slot_ids[None, :]).astype(jnp.bfloat16)
        back_pick = back_pick + col_pick
        out_rows = matmul(col_pick, returned)
        layer_sum = layer_sum + gate_grid[:, col : col + 1] * out_rows
        gate_cols.append(jnp.sum(out_grad.astype(jnp.float32) * out_rows, axis=1))
    layer_out = layer_sum.astype(jnp.bfloat16)
    gate_cols.extend(
        [jnp.zeros((tok_count,), jnp.float32)] * (top_count - live_cols)
    )
    gates_grad = jnp.stack(gate_cols, axis=1)

    share = gate_mat.shape[0] // lax.axis_size("rep")
    start = lax.axis_index("rep") * share
    gate_share = lax.dynamic_slice_in_dim(gate_mat, start, share, axis=0)
    up_share = lax.dynamic_slice_in_dim(up_mat, start, share, axis=0)
    down_share = lax.dynamic_slice_in_dim(down_mat, start, share, axis=0)
    rows_all = gathered[:, :feature_width]
    grad_all = gathered[:, feature_width:]
    pre_both = rows_times(rows_all, jnp.concatenate([gate_share, up_share], axis=0))
    pre_gate_s = pre_both[:, :share]
    pre_up_s = pre_both[:, share:]
    activated_s = jax.nn.silu(pre_gate_s)
    hidden_s = (activated_s * pre_up_s).astype(jnp.bfloat16)
    hidden_grad_s = rows_times(grad_all, down_share)
    gate_pre_grad_s = (hidden_grad_s * pre_up_s * silu_grad(pre_gate_s)).astype(jnp.bfloat16)
    up_pre_grad_s = (hidden_grad_s * activated_s).astype(jnp.bfloat16)
    both_w_grad = inner_rows(
        jnp.concatenate([gate_pre_grad_s, up_pre_grad_s], axis=1), rows_all
    ).astype(jnp.bfloat16)
    gate_w_grad = both_w_grad[:share][None]
    up_w_grad = both_w_grad[share:][None]
    down_w_grad = inner_rows(hidden_s, grad_all).astype(jnp.bfloat16)[None]
    part_back, gate_w_grad, up_w_grad, down_w_grad = lax.optimization_barrier(
        (part_back, gate_w_grad, up_w_grad, down_w_grad)
    )
    tokens_grad = matmul(back_pick, part_back).astype(jnp.bfloat16)
    return (layer_out, tokens_grad, gates_grad, gate_w_grad, up_w_grad, down_w_grad)


def solution(mesh):
    return jax.shard_map(
        body,
        mesh=mesh,
        in_specs=(
            P(("rep", "ep"), None),
            P(("rep", "ep"), None),
            P(("rep", "ep"), None),
            P("ep", None, None),
            P("ep", None, None),
            P("ep", None, None),
            P(("rep", "ep"), None),
        ),
        out_specs=(
            P(("rep", "ep"), None),
            P(("rep", "ep"), None),
            P(("rep", "ep"), None),
            P("ep", "rep", None),
            P("ep", "rep", None),
            P("ep", "rep", None),
        ),
        check_vma=False,
    )
```

```python
import jax
import jax.numpy as jnp
from jax import lax
from jax.sharding import PartitionSpec as P

STRIPE = 16


def silu_grad(value):
    sigmoid_value = jax.nn.sigmoid(value)
    return sigmoid_value * (1.0 + value * (1.0 - sigmoid_value))


def rows_times(left, right):
    return lax.dot_general(
        left, right, (((1,), (1,)), ((), ())), preferred_element_type=jnp.float32
    )


def inner_rows(left, right):
    return lax.dot_general(
        left, right, (((0,), (0,)), ((), ())), preferred_element_type=jnp.float32
    )


def matmul(left, right):
    return jnp.dot(left, right, preferred_element_type=jnp.float32)


def body(tokens, expert_ids, gate_weights, w_gate, w_up, w_down, out_grad):
    tok_count, feature_width = tokens.shape
    top_count = expert_ids.shape[1]
    experts = lax.axis_size("ep")
    per_pair = tok_count // 8
    total_slots = experts * per_pair
    live_cols = min(top_count, -(-experts // STRIPE))
    assigned = tok_count * live_cols

    flat_ids = expert_ids[:, :live_cols].reshape(-1)
    flat_gates = gate_weights[:, :live_cols].reshape(-1)
    live_mask = flat_ids < experts
    onehot = flat_ids[:, None] == jnp.arange(experts, dtype=jnp.int32)[None, :]
    position = jnp.arange(assigned, dtype=jnp.int32)
    earlier = (position[:, None] > position[None, :]).astype(jnp.bfloat16)
    before = matmul(earlier, onehot.astype(jnp.bfloat16))
    slot_rank = jnp.sum(jnp.where(onehot, before, 0.0), axis=1).astype(jnp.int32)
    slot_index = jnp.where(live_mask, flat_ids * per_pair + slot_rank, -1)

    slot_ids = jnp.arange(total_slots, dtype=jnp.int32)
    hit = slot_ids[:, None] == slot_index[None, :]
    slot_gate = jnp.sum(jnp.where(hit, flat_gates[None, :], 0.0), axis=1)
    pick = jnp.any(hit.reshape(total_slots, tok_count, live_cols), axis=2).astype(jnp.bfloat16)
    send_rows = matmul(pick, tokens).astype(jnp.bfloat16)
    grad_rows = matmul(pick, out_grad)
    scaled_grad = (slot_gate[:, None] * grad_rows).astype(jnp.bfloat16)

    outgoing = jnp.concatenate([send_rows, scaled_grad], axis=1)
    received = lax.all_to_all(
        outgoing.reshape(experts, per_pair, 2 * feature_width),
        "ep",
        split_axis=0,
        concat_axis=0,
        tiled=True,
    ).reshape(total_slots, 2 * feature_width)

    copies = lax.axis_size("rep")
    if copies == 4:
        far = lax.ppermute(received, "rep", [(r, r ^ 2) for r in range(copies)])
    else:
        gathered = lax.all_gather(received, "rep", axis=0, tiled=True)

    rows_in = received[:, :feature_width]
    grad_in = received[:, feature_width:]
    gate_mat = w_gate[0]
    up_mat = w_up[0]
    down_mat = w_down[0]
    pre_gate = rows_times(rows_in, gate_mat)
    pre_up = rows_times(rows_in, up_mat)
    activated = jax.nn.silu(pre_gate)
    hidden = (activated * pre_up).astype(jnp.bfloat16)
    expert_out = matmul(hidden, down_mat).astype(jnp.bfloat16)
    expert_out, grad_in = lax.optimization_barrier((expert_out, grad_in))
    returned = lax.all_to_all(
        expert_out.reshape(experts, per_pair, feature_width),
        "ep",
        split_axis=0,
        concat_axis=0,
        tiled=True,
    ).reshape(total_slots, feature_width)

    hidden_grad = rows_times(grad_in, down_mat)
    gate_pre_grad = (hidden_grad * pre_up * silu_grad(pre_gate)).astype(jnp.bfloat16)
    up_pre_grad = (hidden_grad * activated).astype(jnp.bfloat16)
    token_part = (
        matmul(gate_pre_grad, gate_mat) + matmul(up_pre_grad, up_mat)
    ).astype(jnp.bfloat16)
    part_back = lax.all_to_all(
        token_part.reshape(experts, per_pair, feature_width),
        "ep",
        split_axis=0,
        concat_axis=0,
        tiled=True,
    ).reshape(total_slots, feature_width)

    if copies == 4:
        returned, far = lax.optimization_barrier((returned, far))
        pair = jnp.concatenate([received, far], axis=0)
        near = lax.ppermute(pair, "rep", [(r, r ^ 1) for r in range(copies)])
        gathered = jnp.concatenate([pair, near], axis=0)
    slot_grid = slot_index.reshape(tok_count, live_cols)
    gate_grid = flat_gates.reshape(tok_count, live_cols)
    layer_sum = jnp.zeros((tok_count, feature_width), jnp.float32)
    gate_cols = []
    back_pick = jnp.zeros((tok_count, total_slots), jnp.bfloat16)
    for col in range(live_cols):
        col_pick = (slot_grid[:, col : col + 1] == slot_ids[None, :]).astype(jnp.bfloat16)
        back_pick = back_pick + col_pick
        out_rows = matmul(col_pick, returned)
        layer_sum = layer_sum + gate_grid[:, col : col + 1] * out_rows
        gate_cols.append(jnp.sum(out_grad.astype(jnp.float32) * out_rows, axis=1))
    layer_out = layer_sum.astype(jnp.bfloat16)
    gate_cols.extend(
        [jnp.zeros((tok_count,), jnp.float32)] * (top_count - live_cols)
    )
    gates_grad = jnp.stack(gate_cols, axis=1)

    share = gate_mat.shape[0] // copies
    start = lax.axis_index("rep") * share
    gate_share = lax.dynamic_slice_in_dim(gate_mat, start, share, axis=0)
    up_share = lax.dynamic_slice_in_dim(up_mat, start, share, axis=0)
    down_share = lax.dynamic_slice_in_dim(down_mat, start, share, axis=0)
    rows_all = gathered[:, :feature_width]
    grad_all = gathered[:, feature_width:]
    pre_both = rows_times(rows_all, jnp.concatenate([gate_share, up_share], axis=0))
    pre_gate_s = pre_both[:, :share]
    pre_up_s = pre_both[:, share:]
    activated_s = jax.nn.silu(pre_gate_s)
    hidden_s = (activated_s * pre_up_s).astype(jnp.bfloat16)
    hidden_grad_s = rows_times(grad_all, down_share)
    gate_pre_grad_s = (hidden_grad_s * pre_up_s * silu_grad(pre_gate_s)).astype(jnp.bfloat16)
    up_pre_grad_s = (hidden_grad_s * activated_s).astype(jnp.bfloat16)
    both_w_grad = inner_rows(
        jnp.concatenate([gate_pre_grad_s, up_pre_grad_s], axis=1), rows_all
    ).astype(jnp.bfloat16)
    gate_w_grad = both_w_grad[:share][None]
    up_w_grad = both_w_grad[share:][None]
    down_w_grad = inner_rows(hidden_s, grad_all).astype(jnp.bfloat16)[None]
    part_back, gate_w_grad, up_w_grad, down_w_grad = lax.optimization_barrier(
        (part_back, gate_w_grad, up_w_grad, down_w_grad)
    )
    tokens_grad = matmul(back_pick, part_back).astype(jnp.bfloat16)
    return (layer_out, tokens_grad, gates_grad, gate_w_grad, up_w_grad, down_w_grad)


def solution(mesh):
    return jax.shard_map(
        body,
        mesh=mesh,
        in_specs=(
            P(("rep", "ep"), None),
            P(("rep", "ep"), None),
            P(("rep", "ep"), None),
            P("ep", None, None),
            P("ep", None, None),
            P("ep", None, None),
            P(("rep", "ep"), None),
        ),
        out_specs=(
            P(("rep", "ep"), None),
            P(("rep", "ep"), None),
            P(("rep", "ep"), None),
            P("ep", "rep", None),
            P("ep", "rep", None),
            P("ep", "rep", None),
        ),
        check_vma=False,
    )
```

```python
import jax
import jax.numpy as jnp
from jax import lax
from jax.sharding import PartitionSpec as P

STRIPE = 16


def silu_grad(value):
    sigmoid_value = jax.nn.sigmoid(value)
    return sigmoid_value * (1.0 + value * (1.0 - sigmoid_value))


def rows_times(left, right):
    return lax.dot_general(
        left, right, (((1,), (1,)), ((), ())), preferred_element_type=jnp.float32
    )


def inner_rows(left, right):
    return lax.dot_general(
        left, right, (((0,), (0,)), ((), ())), preferred_element_type=jnp.float32
    )


def matmul(left, right):
    return jnp.dot(left, right, preferred_element_type=jnp.float32)


def body(tokens, expert_ids, gate_weights, w_gate, w_up, w_down, out_grad):
    tok_count, feature_width = tokens.shape
    top_count = expert_ids.shape[1]
    experts = lax.axis_size("ep")
    per_pair = tok_count // 8
    total_slots = experts * per_pair
    live_cols = min(top_count, -(-experts // STRIPE))
    assigned = tok_count * live_cols

    flat_ids = expert_ids[:, :live_cols].reshape(-1)
    flat_gates = gate_weights[:, :live_cols].reshape(-1)
    live_mask = flat_ids < experts
    onehot = flat_ids[:, None] == jnp.arange(experts, dtype=jnp.int32)[None, :]
    position = jnp.arange(assigned, dtype=jnp.int32)
    earlier = (position[:, None] > position[None, :]).astype(jnp.bfloat16)
    before = matmul(earlier, onehot.astype(jnp.bfloat16))
    slot_rank = jnp.sum(jnp.where(onehot, before, 0.0), axis=1).astype(jnp.int32)
    slot_index = jnp.where(live_mask, flat_ids * per_pair + slot_rank, -1)

    slot_ids = jnp.arange(total_slots, dtype=jnp.int32)
    hit = slot_ids[:, None] == slot_index[None, :]
    slot_gate = jnp.sum(jnp.where(hit, flat_gates[None, :], 0.0), axis=1)
    pick = jnp.any(hit.reshape(total_slots, tok_count, live_cols), axis=2).astype(jnp.bfloat16)
    send_rows = matmul(pick, tokens).astype(jnp.bfloat16)
    grad_rows = matmul(pick, out_grad)
    scaled_grad = (slot_gate[:, None] * grad_rows).astype(jnp.bfloat16)

    outgoing = jnp.concatenate([send_rows, scaled_grad], axis=1)
    received = lax.all_to_all(
        outgoing.reshape(experts, per_pair, 2 * feature_width),
        "ep",
        split_axis=0,
        concat_axis=0,
        tiled=True,
    ).reshape(total_slots, 2 * feature_width)

    copies = lax.axis_size("rep")
    by_pieces = copies == 4
    if by_pieces:
        near = lax.ppermute(received, "rep", [(r, r ^ 1) for r in range(copies)])
        far = lax.ppermute(received, "rep", [(r, r ^ 2) for r in range(copies)])
    else:
        gathered = lax.all_gather(received, "rep", axis=0, tiled=True)

    rows_in = received[:, :feature_width]
    grad_in = received[:, feature_width:]
    gate_mat = w_gate[0]
    up_mat = w_up[0]
    down_mat = w_down[0]
    pre_gate = rows_times(rows_in, gate_mat)
    pre_up = rows_times(rows_in, up_mat)
    activated = jax.nn.silu(pre_gate)
    hidden = (activated * pre_up).astype(jnp.bfloat16)
    expert_out = matmul(hidden, down_mat).astype(jnp.bfloat16)
    returned = lax.all_to_all(
        expert_out.reshape(experts, per_pair, feature_width),
        "ep",
        split_axis=0,
        concat_axis=0,
        tiled=True,
    ).reshape(total_slots, feature_width)

    hidden_grad = rows_times(grad_in, down_mat)
    gate_pre_grad = (hidden_grad * pre_up * silu_grad(pre_gate)).astype(jnp.bfloat16)
    up_pre_grad = (hidden_grad * activated).astype(jnp.bfloat16)
    token_part = (
        matmul(gate_pre_grad, gate_mat) + matmul(up_pre_grad, up_mat)
    ).astype(jnp.bfloat16)
    part_back = lax.all_to_all(
        token_part.reshape(experts, per_pair, feature_width),
        "ep",
        split_axis=0,
        concat_axis=0,
        tiled=True,
    ).reshape(total_slots, feature_width)

    if by_pieces:
        returned, near = lax.optimization_barrier((returned, near))
    slot_grid = slot_index.reshape(tok_count, live_cols)
    gate_grid = flat_gates.reshape(tok_count, live_cols)
    layer_sum = jnp.zeros((tok_count, feature_width), jnp.float32)
    gate_cols = []
    back_pick = jnp.zeros((tok_count, total_slots), jnp.bfloat16)
    for col in range(live_cols):
        col_pick = (slot_grid[:, col : col + 1] == slot_ids[None, :]).astype(jnp.bfloat16)
        back_pick = back_pick + col_pick
        out_rows = matmul(col_pick, returned)
        layer_sum = layer_sum + gate_grid[:, col : col + 1] * out_rows
        gate_cols.append(jnp.sum(out_grad.astype(jnp.float32) * out_rows, axis=1))
    if by_pieces:
        layer_sum, far = lax.optimization_barrier((layer_sum, far))
        near_far = lax.ppermute(far, "rep", [(r, r ^ 1) for r in range(copies)])
        pieces = [received, near, far, near_far]
    else:
        pieces = [gathered]
    layer_out = layer_sum.astype(jnp.bfloat16)
    gate_cols.extend(
        [jnp.zeros((tok_count,), jnp.float32)] * (top_count - live_cols)
    )
    gates_grad = jnp.stack(gate_cols, axis=1)

    share = gate_mat.shape[0] // copies
    start = lax.axis_index("rep") * share
    gate_share = lax.dynamic_slice_in_dim(gate_mat, start, share, axis=0)
    up_share = lax.dynamic_slice_in_dim(up_mat, start, share, axis=0)
    down_share = lax.dynamic_slice_in_dim(down_mat, start, share, axis=0)
    both_sum = None
    down_sum = None
    stacked_share = jnp.concatenate([gate_share, up_share], axis=0)
    for piece in pieces:
        rows_p = piece[:, :feature_width]
        grad_p = piece[:, feature_width:]
        pre_both = rows_times(rows_p, stacked_share)
        pre_gate_s = pre_both[:, :share]
        pre_up_s = pre_both[:, share:]
        activated_s = jax.nn.silu(pre_gate_s)
        hidden_s = (activated_s * pre_up_s).astype(jnp.bfloat16)
        hidden_grad_s = rows_times(grad_p, down_share)
        gate_pre_grad_s = (hidden_grad_s * pre_up_s * silu_grad(pre_gate_s)).astype(jnp.bfloat16)
        up_pre_grad_s = (hidden_grad_s * activated_s).astype(jnp.bfloat16)
        both_p = inner_rows(jnp.concatenate([gate_pre_grad_s, up_pre_grad_s], axis=1), rows_p)
        down_p = inner_rows(hidden_s, grad_p)
        both_sum = both_p if both_sum is None else both_sum + both_p
        down_sum = down_p if down_sum is None else down_sum + down_p
    gate_w_grad = both_sum[:share].astype(jnp.bfloat16)[None]
    up_w_grad = both_sum[share:].astype(jnp.bfloat16)[None]
    down_w_grad = down_sum.astype(jnp.bfloat16)[None]
    part_back, gate_w_grad, up_w_grad, down_w_grad = lax.optimization_barrier(
        (part_back, gate_w_grad, up_w_grad, down_w_grad)
    )
    tokens_grad = matmul(back_pick, part_back).astype(jnp.bfloat16)
    return (layer_out, tokens_grad, gates_grad, gate_w_grad, up_w_grad, down_w_grad)


def solution(mesh):
    return jax.shard_map(
        body,
        mesh=mesh,
        in_specs=(
            P(("rep", "ep"), None),
            P(("rep", "ep"), None),
            P(("rep", "ep"), None),
            P("ep", None, None),
            P("ep", None, None),
            P("ep", None, None),
            P(("rep", "ep"), None),
        ),
        out_specs=(
            P(("rep", "ep"), None),
            P(("rep", "ep"), None),
            P(("rep", "ep"), None),
            P("ep", "rep", None),
            P("ep", "rep", None),
            P("ep", "rep", None),
        ),
        check_vma=False,
    )
```

```python
import jax
import jax.numpy as jnp
from jax import lax
from jax.sharding import PartitionSpec as P

STRIPE = 16


def silu_grad(value):
    sigmoid_value = jax.nn.sigmoid(value)
    return sigmoid_value * (1.0 + value * (1.0 - sigmoid_value))


def rows_times(left, right):
    return lax.dot_general(
        left, right, (((1,), (1,)), ((), ())), preferred_element_type=jnp.float32
    )


def inner_rows(left, right):
    return lax.dot_general(
        left, right, (((0,), (0,)), ((), ())), preferred_element_type=jnp.float32
    )


def matmul(left, right):
    return jnp.dot(left, right, preferred_element_type=jnp.float32)


def body(tokens, expert_ids, gate_weights, w_gate, w_up, w_down, out_grad):
    tok_count, feature_width = tokens.shape
    top_count = expert_ids.shape[1]
    experts = lax.axis_size("ep")
    per_pair = tok_count // 8
    total_slots = experts * per_pair
    live_cols = min(top_count, -(-experts // STRIPE))
    assigned = tok_count * live_cols

    flat_ids = expert_ids[:, :live_cols].reshape(-1)
    flat_gates = gate_weights[:, :live_cols].reshape(-1)
    live_mask = flat_ids < experts
    onehot = flat_ids[:, None] == jnp.arange(experts, dtype=jnp.int32)[None, :]
    position = jnp.arange(assigned, dtype=jnp.int32)
    earlier = (position[:, None] > position[None, :]).astype(jnp.bfloat16)
    before = matmul(earlier, onehot.astype(jnp.bfloat16))
    slot_rank = jnp.sum(jnp.where(onehot, before, 0.0), axis=1).astype(jnp.int32)
    slot_index = jnp.where(live_mask, flat_ids * per_pair + slot_rank, -1)

    slot_ids = jnp.arange(total_slots, dtype=jnp.int32)
    hit = slot_ids[:, None] == slot_index[None, :]
    slot_gate = jnp.sum(jnp.where(hit, flat_gates[None, :], 0.0), axis=1)
    pick = jnp.any(hit.reshape(total_slots, tok_count, live_cols), axis=2).astype(jnp.bfloat16)
    send_rows = matmul(pick, tokens).astype(jnp.bfloat16)
    grad_rows = matmul(pick, out_grad)
    scaled_grad = (slot_gate[:, None] * grad_rows).astype(jnp.bfloat16)

    outgoing = jnp.concatenate([send_rows, scaled_grad], axis=1)
    received = lax.all_to_all(
        outgoing.reshape(experts, per_pair, 2 * feature_width),
        "ep",
        split_axis=0,
        concat_axis=0,
        tiled=True,
    ).reshape(total_slots, 2 * feature_width)

    copies = lax.axis_size("rep")
    by_pieces = copies == 4
    if by_pieces:
        near = lax.ppermute(received, "rep", [(r, r ^ 1) for r in range(copies)])
        half = total_slots // 2
        far_first = lax.ppermute(received[:half], "rep", [(r, r ^ 2) for r in range(copies)])
        far_second = lax.ppermute(received[half:], "rep", [(r, r ^ 2) for r in range(copies)])
    else:
        gathered = lax.all_gather(received, "rep", axis=0, tiled=True)

    rows_in = received[:, :feature_width]
    grad_in = received[:, feature_width:]
    gate_mat = w_gate[0]
    up_mat = w_up[0]
    down_mat = w_down[0]
    gate_up_mat = jnp.concatenate([gate_mat, up_mat], axis=0)
    hidden_units = gate_mat.shape[0]
    pre_both_own = rows_times(rows_in, gate_up_mat)
    pre_gate = pre_both_own[:, :hidden_units]
    pre_up = pre_both_own[:, hidden_units:]
    activated = jax.nn.silu(pre_gate)
    hidden = (activated * pre_up).astype(jnp.bfloat16)
    expert_out = matmul(hidden, down_mat).astype(jnp.bfloat16)
    returned = lax.all_to_all(
        expert_out.reshape(experts, per_pair, feature_width),
        "ep",
        split_axis=0,
        concat_axis=0,
        tiled=True,
    ).reshape(total_slots, feature_width)

    hidden_grad = rows_times(grad_in, down_mat)
    gate_pre_grad = (hidden_grad * pre_up * silu_grad(pre_gate)).astype(jnp.bfloat16)
    up_pre_grad = (hidden_grad * activated).astype(jnp.bfloat16)
    token_part = matmul(
        jnp.concatenate([gate_pre_grad, up_pre_grad], axis=1), gate_up_mat
    ).astype(jnp.bfloat16)
    part_back = lax.all_to_all(
        token_part.reshape(experts, per_pair, feature_width),
        "ep",
        split_axis=0,
        concat_axis=0,
        tiled=True,
    ).reshape(total_slots, feature_width)

    if by_pieces:
        returned, near, far_first = lax.optimization_barrier((returned, near, far_first))
        near_far_first = lax.ppermute(far_first, "rep", [(r, r ^ 1) for r in range(copies)])
    slot_grid = slot_index.reshape(tok_count, live_cols)
    gate_grid = flat_gates.reshape(tok_count, live_cols)
    layer_sum = jnp.zeros((tok_count, feature_width), jnp.float32)
    gate_cols = []
    back_pick = jnp.zeros((tok_count, total_slots), jnp.bfloat16)
    for col in range(live_cols):
        col_pick = (slot_grid[:, col : col + 1] == slot_ids[None, :]).astype(jnp.bfloat16)
        back_pick = back_pick + col_pick
        out_rows = matmul(col_pick, returned)
        layer_sum = layer_sum + gate_grid[:, col : col + 1] * out_rows
        gate_cols.append(jnp.sum(out_grad.astype(jnp.float32) * out_rows, axis=1))
    if by_pieces:
        layer_sum, far_second = lax.optimization_barrier((layer_sum, far_second))
        near_far_second = lax.ppermute(far_second, "rep", [(r, r ^ 1) for r in range(copies)])
        pieces = [received, near, far_first, near_far_first, far_second, near_far_second]
    else:
        pieces = [gathered]
    layer_out = layer_sum.astype(jnp.bfloat16)
    gate_cols.extend(
        [jnp.zeros((tok_count,), jnp.float32)] * (top_count - live_cols)
    )
    gates_grad = jnp.stack(gate_cols, axis=1)

    share = gate_mat.shape[0] // copies
    start = lax.axis_index("rep") * share
    gate_share = lax.dynamic_slice_in_dim(gate_mat, start, share, axis=0)
    up_share = lax.dynamic_slice_in_dim(up_mat, start, share, axis=0)
    down_share = lax.dynamic_slice_in_dim(down_mat, start, share, axis=0)
    both_sum = None
    down_sum = None
    stacked_share = jnp.concatenate([gate_share, up_share], axis=0)
    for piece in pieces:
        rows_p = piece[:, :feature_width]
        grad_p = piece[:, feature_width:]
        pre_both = rows_times(rows_p, stacked_share)
        pre_gate_s = pre_both[:, :share]
        pre_up_s = pre_both[:, share:]
        activated_s = jax.nn.silu(pre_gate_s)
        hidden_s = (activated_s * pre_up_s).astype(jnp.bfloat16)
        hidden_grad_s = rows_times(grad_p, down_share)
        gate_pre_grad_s = (hidden_grad_s * pre_up_s * silu_grad(pre_gate_s)).astype(jnp.bfloat16)
        up_pre_grad_s = (hidden_grad_s * activated_s).astype(jnp.bfloat16)
        both_p = inner_rows(jnp.concatenate([gate_pre_grad_s, up_pre_grad_s], axis=1), rows_p)
        down_p = inner_rows(hidden_s, grad_p)
        both_sum = both_p if both_sum is None else both_sum + both_p
        down_sum = down_p if down_sum is None else down_sum + down_p
    gate_w_grad = both_sum[:share].astype(jnp.bfloat16)[None]
    up_w_grad = both_sum[share:].astype(jnp.bfloat16)[None]
    down_w_grad = down_sum.astype(jnp.bfloat16)[None]
    part_back, gate_w_grad, up_w_grad, down_w_grad = lax.optimization_barrier(
        (part_back, gate_w_grad, up_w_grad, down_w_grad)
    )
    tokens_grad = matmul(back_pick, part_back).astype(jnp.bfloat16)
    return (layer_out, tokens_grad, gates_grad, gate_w_grad, up_w_grad, down_w_grad)


def solution(mesh):
    return jax.shard_map(
        body,
        mesh=mesh,
        in_specs=(
            P(("rep", "ep"), None),
            P(("rep", "ep"), None),
            P(("rep", "ep"), None),
            P("ep", None, None),
            P("ep", None, None),
            P("ep", None, None),
            P(("rep", "ep"), None),
        ),
        out_specs=(
            P(("rep", "ep"), None),
            P(("rep", "ep"), None),
            P(("rep", "ep"), None),
            P("ep", "rep", None),
            P("ep", "rep", None),
            P("ep", "rep", None),
        ),
        check_vma=False,
    )
```

```python
import jax
import jax.numpy as jnp
from jax import lax
from jax.sharding import PartitionSpec as P

STRIPE = 16


def silu_grad(value):
    sigmoid_value = jax.nn.sigmoid(value)
    return sigmoid_value * (1.0 + value * (1.0 - sigmoid_value))


def rows_times(left, right):
    return lax.dot_general(
        left, right, (((1,), (1,)), ((), ())), preferred_element_type=jnp.float32
    )


def inner_rows(left, right):
    return lax.dot_general(
        left, right, (((0,), (0,)), ((), ())), preferred_element_type=jnp.float32
    )


def matmul(left, right):
    return jnp.dot(left, right, preferred_element_type=jnp.float32)


def body(tokens, expert_ids, gate_weights, w_gate, w_up, w_down, out_grad):
    tok_count, feature_width = tokens.shape
    top_count = expert_ids.shape[1]
    experts = lax.axis_size("ep")
    per_pair = tok_count // 8
    total_slots = experts * per_pair
    live_cols = min(top_count, -(-experts // STRIPE))
    assigned = tok_count * live_cols

    flat_ids = expert_ids[:, :live_cols].reshape(-1)
    flat_gates = gate_weights[:, :live_cols].reshape(-1)
    live_mask = flat_ids < experts
    onehot = flat_ids[:, None] == jnp.arange(experts, dtype=jnp.int32)[None, :]
    position = jnp.arange(assigned, dtype=jnp.int32)
    earlier = (position[:, None] > position[None, :]).astype(jnp.bfloat16)
    before = matmul(earlier, onehot.astype(jnp.bfloat16))
    slot_rank = jnp.sum(jnp.where(onehot, before, 0.0), axis=1).astype(jnp.int32)
    slot_index = jnp.where(live_mask, flat_ids * per_pair + slot_rank, -1)

    slot_ids = jnp.arange(total_slots, dtype=jnp.int32)
    hit = slot_ids[:, None] == slot_index[None, :]
    slot_gate = jnp.sum(jnp.where(hit, flat_gates[None, :], 0.0), axis=1)
    pick = jnp.any(hit.reshape(total_slots, tok_count, live_cols), axis=2).astype(jnp.bfloat16)
    send_rows = matmul(pick, tokens).astype(jnp.bfloat16)
    grad_rows = matmul(pick, out_grad)
    scaled_grad = (slot_gate[:, None] * grad_rows).astype(jnp.bfloat16)

    outgoing = jnp.concatenate([send_rows, scaled_grad], axis=1)
    received = lax.all_to_all(
        outgoing.reshape(experts, per_pair, 2 * feature_width),
        "ep",
        split_axis=0,
        concat_axis=0,
        tiled=True,
    ).reshape(total_slots, 2 * feature_width)

    copies = lax.axis_size("rep")
    by_pieces = copies == 4
    if by_pieces:
        near = lax.ppermute(received, "rep", [(r, r ^ 1) for r in range(copies)])
        far = lax.ppermute(received, "rep", [(r, r ^ 2) for r in range(copies)])
    else:
        gathered = lax.all_gather(received, "rep", axis=0, tiled=True)

    rows_in = received[:, :feature_width]
    grad_in = received[:, feature_width:]
    gate_mat = w_gate[0]
    up_mat = w_up[0]
    down_mat = w_down[0]
    gate_up_mat = jnp.concatenate([gate_mat, up_mat], axis=0)
    hidden_units = gate_mat.shape[0]
    pre_both_own = rows_times(rows_in, gate_up_mat)
    pre_gate = pre_both_own[:, :hidden_units]
    pre_up = pre_both_own[:, hidden_units:]
    activated = jax.nn.silu(pre_gate)
    hidden = (activated * pre_up).astype(jnp.bfloat16)
    expert_out = matmul(hidden, down_mat).astype(jnp.bfloat16)
    returned = lax.all_to_all(
        expert_out.reshape(experts, per_pair, feature_width),
        "ep",
        split_axis=0,
        concat_axis=0,
        tiled=True,
    ).reshape(total_slots, feature_width)

    hidden_grad = rows_times(grad_in, down_mat)
    gate_pre_grad = (hidden_grad * pre_up * silu_grad(pre_gate)).astype(jnp.bfloat16)
    up_pre_grad = (hidden_grad * activated).astype(jnp.bfloat16)
    token_part = matmul(
        jnp.concatenate([gate_pre_grad, up_pre_grad], axis=1), gate_up_mat
    ).astype(jnp.bfloat16)
    part_back = lax.all_to_all(
        token_part.reshape(experts, per_pair, feature_width),
        "ep",
        split_axis=0,
        concat_axis=0,
        tiled=True,
    ).reshape(total_slots, feature_width)

    if by_pieces:
        returned, near = lax.optimization_barrier((returned, near))
    slot_grid = slot_index.reshape(tok_count, live_cols)
    gate_grid = flat_gates.reshape(tok_count, live_cols)
    layer_sum = jnp.zeros((tok_count, feature_width), jnp.float32)
    gate_cols = []
    back_pick = jnp.zeros((tok_count, total_slots), jnp.bfloat16)
    for col in range(live_cols):
        col_pick = (slot_grid[:, col : col + 1] == slot_ids[None, :]).astype(jnp.bfloat16)
        back_pick = back_pick + col_pick
        out_rows = matmul(col_pick, returned)
        layer_sum = layer_sum + gate_grid[:, col : col + 1] * out_rows
        gate_cols.append(jnp.sum(out_grad.astype(jnp.float32) * out_rows, axis=1))
    if by_pieces:
        layer_sum, far = lax.optimization_barrier((layer_sum, far))
        near_far = lax.ppermute(far, "rep", [(r, r ^ 1) for r in range(copies)])
        pieces = [received, near, far, near_far]
    else:
        pieces = [gathered]
    layer_out = layer_sum.astype(jnp.bfloat16)
    gate_cols.extend(
        [jnp.zeros((tok_count,), jnp.float32)] * (top_count - live_cols)
    )
    gates_grad = jnp.stack(gate_cols, axis=1)

    share = gate_mat.shape[0] // copies
    start = lax.axis_index("rep") * share
    gate_share = lax.dynamic_slice_in_dim(gate_mat, start, share, axis=0)
    up_share = lax.dynamic_slice_in_dim(up_mat, start, share, axis=0)
    down_share = lax.dynamic_slice_in_dim(down_mat, start, share, axis=0)
    both_sum = None
    down_sum = None
    stacked_share = jnp.concatenate([gate_share, up_share], axis=0)
    for piece in pieces:
        rows_p = piece[:, :feature_width]
        grad_p = piece[:, feature_width:]
        pre_both = rows_times(rows_p, stacked_share)
        pre_gate_s = pre_both[:, :share]
        pre_up_s = pre_both[:, share:]
        activated_s = jax.nn.silu(pre_gate_s)
        hidden_s = (activated_s * pre_up_s).astype(jnp.bfloat16)
        hidden_grad_s = rows_times(grad_p, down_share)
        gate_pre_grad_s = (hidden_grad_s * pre_up_s * silu_grad(pre_gate_s)).astype(jnp.bfloat16)
        up_pre_grad_s = (hidden_grad_s * activated_s).astype(jnp.bfloat16)
        both_p = inner_rows(jnp.concatenate([gate_pre_grad_s, up_pre_grad_s], axis=1), rows_p)
        down_p = inner_rows(hidden_s, grad_p)
        both_sum = both_p if both_sum is None else both_sum + both_p
        down_sum = down_p if down_sum is None else down_sum + down_p
    gate_w_grad = both_sum[:share].astype(jnp.bfloat16)[None]
    up_w_grad = both_sum[share:].astype(jnp.bfloat16)[None]
    down_w_grad = down_sum.astype(jnp.bfloat16)[None]
    part_back, gate_w_grad, up_w_grad, down_w_grad = lax.optimization_barrier(
        (part_back, gate_w_grad, up_w_grad, down_w_grad)
    )
    tokens_grad = matmul(back_pick, part_back).astype(jnp.bfloat16)
    return (layer_out, tokens_grad, gates_grad, gate_w_grad, up_w_grad, down_w_grad)


def solution(mesh):
    return jax.shard_map(
        body,
        mesh=mesh,
        in_specs=(
            P(("rep", "ep"), None),
            P(("rep", "ep"), None),
            P(("rep", "ep"), None),
            P("ep", None, None),
            P("ep", None, None),
            P("ep", None, None),
            P(("rep", "ep"), None),
        ),
        out_specs=(
            P(("rep", "ep"), None),
            P(("rep", "ep"), None),
            P(("rep", "ep"), None),
            P("ep", "rep", None),
            P("ep", "rep", None),
            P("ep", "rep", None),
        ),
        check_vma=False,
    )
```

```python
import jax
import jax.numpy as jnp
from jax import lax
from jax.sharding import PartitionSpec as P

STRIPE = 16


def silu_grad(value):
    sigmoid_value = jax.nn.sigmoid(value)
    return sigmoid_value * (1.0 + value * (1.0 - sigmoid_value))


def rows_times(left, right):
    return lax.dot_general(
        left, right, (((1,), (1,)), ((), ())), preferred_element_type=jnp.float32
    )


def inner_rows(left, right):
    return lax.dot_general(
        left, right, (((0,), (0,)), ((), ())), preferred_element_type=jnp.float32
    )


def matmul(left, right):
    return jnp.dot(left, right, preferred_element_type=jnp.float32)


def body(tokens, expert_ids, gate_weights, w_gate, w_up, w_down, out_grad):
    tok_count, feature_width = tokens.shape
    top_count = expert_ids.shape[1]
    experts = lax.axis_size("ep")
    per_pair = tok_count // 8
    total_slots = experts * per_pair
    live_cols = min(top_count, -(-experts // STRIPE))
    assigned = tok_count * live_cols

    flat_ids = expert_ids[:, :live_cols].reshape(-1)
    flat_gates = gate_weights[:, :live_cols].reshape(-1)
    live_mask = flat_ids < experts
    onehot = flat_ids[:, None] == jnp.arange(experts, dtype=jnp.int32)[None, :]
    position = jnp.arange(assigned, dtype=jnp.int32)
    earlier = (position[:, None] > position[None, :]).astype(jnp.bfloat16)
    before = matmul(earlier, onehot.astype(jnp.bfloat16))
    slot_rank = jnp.sum(jnp.where(onehot, before, 0.0), axis=1).astype(jnp.int32)
    slot_index = jnp.where(live_mask, flat_ids * per_pair + slot_rank, -1)

    slot_ids = jnp.arange(total_slots, dtype=jnp.int32)
    hit = slot_ids[:, None] == slot_index[None, :]
    slot_gate = jnp.sum(jnp.where(hit, flat_gates[None, :], 0.0), axis=1)
    pick = jnp.any(hit.reshape(total_slots, tok_count, live_cols), axis=2).astype(jnp.bfloat16)
    picked = matmul(pick, jnp.concatenate([tokens, out_grad], axis=1))
    column = jnp.arange(2 * feature_width, dtype=jnp.int32)[None, :]
    row_scale = jnp.where(column < feature_width, 1.0, slot_gate[:, None])
    outgoing = (row_scale * picked).astype(jnp.bfloat16)
    received = lax.all_to_all(
        outgoing.reshape(experts, per_pair, 2 * feature_width),
        "ep",
        split_axis=0,
        concat_axis=0,
        tiled=True,
    ).reshape(total_slots, 2 * feature_width)

    copies = lax.axis_size("rep")
    by_pieces = copies == 4
    if by_pieces:
        near = lax.ppermute(received, "rep", [(r, r ^ 1) for r in range(copies)])
        far = lax.ppermute(received, "rep", [(r, r ^ 2) for r in range(copies)])
    else:
        gathered = lax.all_gather(received, "rep", axis=0, tiled=True)

    rows_in = received[:, :feature_width]
    grad_in = received[:, feature_width:]
    gate_mat = w_gate[0]
    up_mat = w_up[0]
    down_mat = w_down[0]
    gate_up_mat = jnp.concatenate([gate_mat, up_mat], axis=0)
    hidden_units = gate_mat.shape[0]
    pre_both_own = rows_times(rows_in, gate_up_mat)
    pre_gate = pre_both_own[:, :hidden_units]
    pre_up = pre_both_own[:, hidden_units:]
    activated = jax.nn.silu(pre_gate)
    hidden = (activated * pre_up).astype(jnp.bfloat16)
    expert_out = matmul(hidden, down_mat).astype(jnp.bfloat16)
    returned = lax.all_to_all(
        expert_out.reshape(experts, per_pair, feature_width),
        "ep",
        split_axis=0,
        concat_axis=0,
        tiled=True,
    ).reshape(total_slots, feature_width)

    hidden_grad = rows_times(grad_in, down_mat)
    gate_pre_grad = (hidden_grad * pre_up * silu_grad(pre_gate)).astype(jnp.bfloat16)
    up_pre_grad = (hidden_grad * activated).astype(jnp.bfloat16)
    token_part = matmul(
        jnp.concatenate([gate_pre_grad, up_pre_grad], axis=1), gate_up_mat
    ).astype(jnp.bfloat16)
    part_back = lax.all_to_all(
        token_part.reshape(experts, per_pair, feature_width),
        "ep",
        split_axis=0,
        concat_axis=0,
        tiled=True,
    ).reshape(total_slots, feature_width)

    if by_pieces:
        returned, near = lax.optimization_barrier((returned, near))
    slot_grid = slot_index.reshape(tok_count, live_cols)
    gate_grid = flat_gates.reshape(tok_count, live_cols)
    layer_sum = jnp.zeros((tok_count, feature_width), jnp.float32)
    gate_cols = []
    back_pick = jnp.zeros((tok_count, total_slots), jnp.bfloat16)
    for col in range(live_cols):
        col_pick = (slot_grid[:, col : col + 1] == slot_ids[None, :]).astype(jnp.bfloat16)
        back_pick = back_pick + col_pick
        out_rows = matmul(col_pick, returned)
        layer_sum = layer_sum + gate_grid[:, col : col + 1] * out_rows
        gate_cols.append(jnp.sum(out_grad.astype(jnp.float32) * out_rows, axis=1))
    if by_pieces:
        layer_sum, far = lax.optimization_barrier((layer_sum, far))
        near_far = lax.ppermute(far, "rep", [(r, r ^ 1) for r in range(copies)])
        pieces = [received, near, far, near_far]
    else:
        pieces = [gathered]
    layer_out = layer_sum.astype(jnp.bfloat16)
    gate_cols.extend(
        [jnp.zeros((tok_count,), jnp.float32)] * (top_count - live_cols)
    )
    gates_grad = jnp.stack(gate_cols, axis=1)

    share = gate_mat.shape[0] // copies
    start = lax.axis_index("rep") * share
    gate_share = lax.dynamic_slice_in_dim(gate_mat, start, share, axis=0)
    up_share = lax.dynamic_slice_in_dim(up_mat, start, share, axis=0)
    down_share = lax.dynamic_slice_in_dim(down_mat, start, share, axis=0)
    both_sum = None
    down_sum = None
    stacked_share = jnp.concatenate([gate_share, up_share], axis=0)
    for piece in pieces:
        rows_p = piece[:, :feature_width]
        grad_p = piece[:, feature_width:]
        pre_both = rows_times(rows_p, stacked_share)
        pre_gate_s = pre_both[:, :share]
        pre_up_s = pre_both[:, share:]
        activated_s = jax.nn.silu(pre_gate_s)
        hidden_s = (activated_s * pre_up_s).astype(jnp.bfloat16)
        hidden_grad_s = rows_times(grad_p, down_share)
        gate_pre_grad_s = (hidden_grad_s * pre_up_s * silu_grad(pre_gate_s)).astype(jnp.bfloat16)
        up_pre_grad_s = (hidden_grad_s * activated_s).astype(jnp.bfloat16)
        both_p = inner_rows(jnp.concatenate([gate_pre_grad_s, up_pre_grad_s], axis=1), rows_p)
        down_p = inner_rows(hidden_s, grad_p)
        both_sum = both_p if both_sum is None else both_sum + both_p
        down_sum = down_p if down_sum is None else down_sum + down_p
    gate_w_grad = both_sum[:share].astype(jnp.bfloat16)[None]
    up_w_grad = both_sum[share:].astype(jnp.bfloat16)[None]
    down_w_grad = down_sum.astype(jnp.bfloat16)[None]
    part_back, gate_w_grad, up_w_grad, down_w_grad = lax.optimization_barrier(
        (part_back, gate_w_grad, up_w_grad, down_w_grad)
    )
    tokens_grad = matmul(back_pick, part_back).astype(jnp.bfloat16)
    return (layer_out, tokens_grad, gates_grad, gate_w_grad, up_w_grad, down_w_grad)


def solution(mesh):
    return jax.shard_map(
        body,
        mesh=mesh,
        in_specs=(
            P(("rep", "ep"), None),
            P(("rep", "ep"), None),
            P(("rep", "ep"), None),
            P("ep", None, None),
            P("ep", None, None),
            P("ep", None, None),
            P(("rep", "ep"), None),
        ),
        out_specs=(
            P(("rep", "ep"), None),
            P(("rep", "ep"), None),
            P(("rep", "ep"), None),
            P("ep", "rep", None),
            P("ep", "rep", None),
            P("ep", "rep", None),
        ),
        check_vma=False,
    )
```

```python
import jax
import jax.numpy as jnp
from jax import lax
from jax.sharding import PartitionSpec as P

STRIPE = 16


def silu_grad(value):
    sigmoid_value = jax.nn.sigmoid(value)
    return sigmoid_value * (1.0 + value * (1.0 - sigmoid_value))


def rows_times(left, right):
    return lax.dot_general(
        left, right, (((1,), (1,)), ((), ())), preferred_element_type=jnp.float32
    )


def inner_rows(left, right):
    return lax.dot_general(
        left, right, (((0,), (0,)), ((), ())), preferred_element_type=jnp.float32
    )


def matmul(left, right):
    return jnp.dot(left, right, preferred_element_type=jnp.float32)


def body(tokens, expert_ids, gate_weights, w_gate, w_up, w_down, out_grad):
    tok_count, feature_width = tokens.shape
    top_count = expert_ids.shape[1]
    experts = lax.axis_size("ep")
    per_pair = tok_count // 8
    total_slots = experts * per_pair
    live_cols = min(top_count, -(-experts // STRIPE))
    assigned = tok_count * live_cols

    flat_ids = expert_ids[:, :live_cols].reshape(-1)
    flat_gates = gate_weights[:, :live_cols].reshape(-1)
    live_mask = flat_ids < experts
    onehot = flat_ids[:, None] == jnp.arange(experts, dtype=jnp.int32)[None, :]
    position = jnp.arange(assigned, dtype=jnp.int32)
    earlier = (position[:, None] > position[None, :]).astype(jnp.bfloat16)
    before = matmul(earlier, onehot.astype(jnp.bfloat16))
    slot_rank = jnp.sum(jnp.where(onehot, before, 0.0), axis=1).astype(jnp.int32)
    slot_index = jnp.where(live_mask, flat_ids * per_pair + slot_rank, -1)

    slot_ids = jnp.arange(total_slots, dtype=jnp.int32)
    hit = slot_ids[:, None] == slot_index[None, :]
    slot_gate = jnp.sum(jnp.where(hit, flat_gates[None, :], 0.0), axis=1)
    pick = jnp.any(hit.reshape(total_slots, tok_count, live_cols), axis=2).astype(jnp.bfloat16)
    send_rows = matmul(pick, tokens).astype(jnp.bfloat16)
    grad_rows = matmul(pick, out_grad)
    scaled_grad = (slot_gate[:, None] * grad_rows).astype(jnp.bfloat16)

    def exchange(rows):
        return lax.all_to_all(
            rows.reshape(experts, per_pair, feature_width),
            "ep",
            split_axis=0,
            concat_axis=0,
            tiled=True,
        ).reshape(total_slots, feature_width)

    rows_in = exchange(send_rows)
    grad_in = exchange(scaled_grad)

    copies = lax.axis_size("rep")
    by_pieces = copies == 4

    def to_copy(values, step):
        return lax.ppermute(values, "rep", [(r, r ^ step) for r in range(copies)])

    if by_pieces:
        far_rows = to_copy(rows_in, 2)
        near_rows = to_copy(rows_in, 1)
    else:
        gathered_rows = lax.all_gather(rows_in, "rep", axis=0, tiled=True)
        gathered_grad = lax.all_gather(grad_in, "rep", axis=0, tiled=True)

    gate_mat = w_gate[0]
    up_mat = w_up[0]
    down_mat = w_down[0]
    gate_up_mat = jnp.concatenate([gate_mat, up_mat], axis=0)
    hidden_units = gate_mat.shape[0]
    pre_both_own = rows_times(rows_in, gate_up_mat)
    pre_gate = pre_both_own[:, :hidden_units]
    pre_up = pre_both_own[:, hidden_units:]
    activated = jax.nn.silu(pre_gate)
    hidden = (activated * pre_up).astype(jnp.bfloat16)
    expert_out = matmul(hidden, down_mat).astype(jnp.bfloat16)
    expert_out, grad_in = lax.optimization_barrier((expert_out, grad_in))
    if by_pieces:
        far_grad = to_copy(grad_in, 2)
        near_grad = to_copy(grad_in, 1)
    returned = lax.all_to_all(
        expert_out.reshape(experts, per_pair, feature_width),
        "ep",
        split_axis=0,
        concat_axis=0,
        tiled=True,
    ).reshape(total_slots, feature_width)

    hidden_grad = rows_times(grad_in, down_mat)
    gate_pre_grad = (hidden_grad * pre_up * silu_grad(pre_gate)).astype(jnp.bfloat16)
    up_pre_grad = (hidden_grad * activated).astype(jnp.bfloat16)
    token_part = matmul(
        jnp.concatenate([gate_pre_grad, up_pre_grad], axis=1), gate_up_mat
    ).astype(jnp.bfloat16)
    part_back = lax.all_to_all(
        token_part.reshape(experts, per_pair, feature_width),
        "ep",
        split_axis=0,
        concat_axis=0,
        tiled=True,
    ).reshape(total_slots, feature_width)

    if by_pieces:
        returned, near_rows, near_grad = lax.optimization_barrier((returned, near_rows, near_grad))
    slot_grid = slot_index.reshape(tok_count, live_cols)
    gate_grid = flat_gates.reshape(tok_count, live_cols)
    layer_sum = jnp.zeros((tok_count, feature_width), jnp.float32)
    gate_cols = []
    back_pick = jnp.zeros((tok_count, total_slots), jnp.bfloat16)
    for col in range(live_cols):
        col_pick = (slot_grid[:, col : col + 1] == slot_ids[None, :]).astype(jnp.bfloat16)
        back_pick = back_pick + col_pick
        out_rows = matmul(col_pick, returned)
        layer_sum = layer_sum + gate_grid[:, col : col + 1] * out_rows
        gate_cols.append(jnp.sum(out_grad.astype(jnp.float32) * out_rows, axis=1))
    if by_pieces:
        layer_sum, far_rows, far_grad = lax.optimization_barrier((layer_sum, far_rows, far_grad))
        pieces = [
            (rows_in, grad_in),
            (near_rows, near_grad),
            (far_rows, far_grad),
            (to_copy(far_rows, 1), to_copy(far_grad, 1)),
        ]
    else:
        pieces = [(gathered_rows, gathered_grad)]
    layer_out = layer_sum.astype(jnp.bfloat16)
    gate_cols.extend(
        [jnp.zeros((tok_count,), jnp.float32)] * (top_count - live_cols)
    )
    gates_grad = jnp.stack(gate_cols, axis=1)

    share = gate_mat.shape[0] // copies
    start = lax.axis_index("rep") * share
    gate_share = lax.dynamic_slice_in_dim(gate_mat, start, share, axis=0)
    up_share = lax.dynamic_slice_in_dim(up_mat, start, share, axis=0)
    down_share = lax.dynamic_slice_in_dim(down_mat, start, share, axis=0)
    both_sum = None
    down_sum = None
    stacked_share = jnp.concatenate([gate_share, up_share], axis=0)
    for rows_p, grad_p in pieces:
        pre_both = rows_times(rows_p, stacked_share)
        pre_gate_s = pre_both[:, :share]
        pre_up_s = pre_both[:, share:]
        activated_s = jax.nn.silu(pre_gate_s)
        hidden_s = (activated_s * pre_up_s).astype(jnp.bfloat16)
        hidden_grad_s = rows_times(grad_p, down_share)
        gate_pre_grad_s = (hidden_grad_s * pre_up_s * silu_grad(pre_gate_s)).astype(jnp.bfloat16)
        up_pre_grad_s = (hidden_grad_s * activated_s).astype(jnp.bfloat16)
        both_p = inner_rows(jnp.concatenate([gate_pre_grad_s, up_pre_grad_s], axis=1), rows_p)
        down_p = inner_rows(hidden_s, grad_p)
        both_sum = both_p if both_sum is None else both_sum + both_p
        down_sum = down_p if down_sum is None else down_sum + down_p
    gate_w_grad = both_sum[:share].astype(jnp.bfloat16)[None]
    up_w_grad = both_sum[share:].astype(jnp.bfloat16)[None]
    down_w_grad = down_sum.astype(jnp.bfloat16)[None]
    part_back, gate_w_grad, up_w_grad, down_w_grad = lax.optimization_barrier(
        (part_back, gate_w_grad, up_w_grad, down_w_grad)
    )
    tokens_grad = matmul(back_pick, part_back).astype(jnp.bfloat16)
    return (layer_out, tokens_grad, gates_grad, gate_w_grad, up_w_grad, down_w_grad)


def solution(mesh):
    return jax.shard_map(
        body,
        mesh=mesh,
        in_specs=(
            P(("rep", "ep"), None),
            P(("rep", "ep"), None),
            P(("rep", "ep"), None),
            P("ep", None, None),
            P("ep", None, None),
            P("ep", None, None),
            P(("rep", "ep"), None),
        ),
        out_specs=(
            P(("rep", "ep"), None),
            P(("rep", "ep"), None),
            P(("rep", "ep"), None),
            P("ep", "rep", None),
            P("ep", "rep", None),
            P("ep", "rep", None),
        ),
        check_vma=False,
    )
```

```python
import jax
import jax.numpy as jnp
from jax import lax
from jax.sharding import PartitionSpec as P

STRIPE = 16


def silu_grad(value):
    sigmoid_value = jax.nn.sigmoid(value)
    return sigmoid_value * (1.0 + value * (1.0 - sigmoid_value))


def rows_times(left, right):
    return lax.dot_general(
        left, right, (((1,), (1,)), ((), ())), preferred_element_type=jnp.float32
    )


def inner_rows(left, right):
    return lax.dot_general(
        left, right, (((0,), (0,)), ((), ())), preferred_element_type=jnp.float32
    )


def matmul(left, right):
    return jnp.dot(left, right, preferred_element_type=jnp.float32)


def body(tokens, expert_ids, gate_weights, w_gate, w_up, w_down, out_grad):
    tok_count, feature_width = tokens.shape
    top_count = expert_ids.shape[1]
    experts = lax.axis_size("ep")
    per_pair = tok_count // 8
    total_slots = experts * per_pair
    live_cols = min(top_count, -(-experts // STRIPE))
    assigned = tok_count * live_cols

    flat_ids = expert_ids[:, :live_cols].reshape(-1)
    flat_gates = gate_weights[:, :live_cols].reshape(-1)
    live_mask = flat_ids < experts
    onehot = flat_ids[:, None] == jnp.arange(experts, dtype=jnp.int32)[None, :]
    position = jnp.arange(assigned, dtype=jnp.int32)
    earlier = (position[:, None] > position[None, :]).astype(jnp.bfloat16)
    before = matmul(earlier, onehot.astype(jnp.bfloat16))
    slot_rank = jnp.sum(jnp.where(onehot, before, 0.0), axis=1).astype(jnp.int32)
    slot_index = jnp.where(live_mask, flat_ids * per_pair + slot_rank, -1)

    slot_ids = jnp.arange(total_slots, dtype=jnp.int32)
    hit = slot_ids[:, None] == slot_index[None, :]
    slot_gate = jnp.sum(jnp.where(hit, flat_gates[None, :], 0.0), axis=1)
    pick = jnp.any(hit.reshape(total_slots, tok_count, live_cols), axis=2).astype(jnp.bfloat16)
    send_rows = matmul(pick, tokens).astype(jnp.bfloat16)
    grad_rows = matmul(pick, out_grad)
    scaled_grad = (slot_gate[:, None] * grad_rows).astype(jnp.bfloat16)

    def exchange(rows):
        return lax.all_to_all(
            rows.reshape(experts, per_pair, feature_width),
            "ep",
            split_axis=0,
            concat_axis=0,
            tiled=True,
        ).reshape(total_slots, feature_width)

    rows_in = exchange(send_rows)
    grad_in = exchange(scaled_grad)

    copies = lax.axis_size("rep")
    by_pieces = copies == 4

    def to_copy(values, step):
        return lax.ppermute(values, "rep", [(r, r ^ step) for r in range(copies)])

    if by_pieces:
        far_rows = to_copy(rows_in, 2)
        near_rows = to_copy(rows_in, 1)
    else:
        gathered_rows = lax.all_gather(rows_in, "rep", axis=0, tiled=True)
        gathered_grad = lax.all_gather(grad_in, "rep", axis=0, tiled=True)

    gate_mat = w_gate[0]
    up_mat = w_up[0]
    down_mat = w_down[0]
    gate_up_mat = jnp.concatenate([gate_mat, up_mat], axis=0)
    hidden_units = gate_mat.shape[0]
    pre_both_own = rows_times(rows_in, gate_up_mat)
    pre_gate = pre_both_own[:, :hidden_units]
    pre_up = pre_both_own[:, hidden_units:]
    activated = jax.nn.silu(pre_gate)
    hidden = (activated * pre_up).astype(jnp.bfloat16)
    expert_out = matmul(hidden, down_mat).astype(jnp.bfloat16)
    expert_out, grad_in = lax.optimization_barrier((expert_out, grad_in))
    returned = lax.all_to_all(
        expert_out.reshape(experts, per_pair, feature_width),
        "ep",
        split_axis=0,
        concat_axis=0,
        tiled=True,
    ).reshape(total_slots, feature_width)

    hidden_grad = rows_times(grad_in, down_mat)
    gate_pre_grad = (hidden_grad * pre_up * silu_grad(pre_gate)).astype(jnp.bfloat16)
    up_pre_grad = (hidden_grad * activated).astype(jnp.bfloat16)
    token_part = matmul(
        jnp.concatenate([gate_pre_grad, up_pre_grad], axis=1), gate_up_mat
    ).astype(jnp.bfloat16)
    if by_pieces:
        token_part, grad_out = lax.optimization_barrier((token_part, grad_in))
        far_grad = to_copy(grad_out, 2)
        near_grad = to_copy(grad_out, 1)
    part_back = lax.all_to_all(
        token_part.reshape(experts, per_pair, feature_width),
        "ep",
        split_axis=0,
        concat_axis=0,
        tiled=True,
    ).reshape(total_slots, feature_width)

    if by_pieces:
        returned, near_rows, near_grad = lax.optimization_barrier((returned, near_rows, near_grad))
    slot_grid = slot_index.reshape(tok_count, live_cols)
    gate_grid = flat_gates.reshape(tok_count, live_cols)
    layer_sum = jnp.zeros((tok_count, feature_width), jnp.float32)
    gate_cols = []
    back_pick = jnp.zeros((tok_count, total_slots), jnp.bfloat16)
    for col in range(live_cols):
        col_pick = (slot_grid[:, col : col + 1] == slot_ids[None, :]).astype(jnp.bfloat16)
        back_pick = back_pick + col_pick
        out_rows = matmul(col_pick, returned)
        layer_sum = layer_sum + gate_grid[:, col : col + 1] * out_rows
        gate_cols.append(jnp.sum(out_grad.astype(jnp.float32) * out_rows, axis=1))
    if by_pieces:
        layer_sum, far_rows, far_grad = lax.optimization_barrier((layer_sum, far_rows, far_grad))
        pieces = [
            (rows_in, grad_in),
            (near_rows, near_grad),
            (far_rows, far_grad),
            (to_copy(far_rows, 1), to_copy(far_grad, 1)),
        ]
    else:
        pieces = [(gathered_rows, gathered_grad)]
    layer_out = layer_sum.astype(jnp.bfloat16)
    gate_cols.extend(
        [jnp.zeros((tok_count,), jnp.float32)] * (top_count - live_cols)
    )
    gates_grad = jnp.stack(gate_cols, axis=1)

    share = gate_mat.shape[0] // copies
    start = lax.axis_index("rep") * share
    gate_share = lax.dynamic_slice_in_dim(gate_mat, start, share, axis=0)
    up_share = lax.dynamic_slice_in_dim(up_mat, start, share, axis=0)
    down_share = lax.dynamic_slice_in_dim(down_mat, start, share, axis=0)
    both_sum = None
    down_sum = None
    stacked_share = jnp.concatenate([gate_share, up_share], axis=0)
    for rows_p, grad_p in pieces:
        pre_both = rows_times(rows_p, stacked_share)
        pre_gate_s = pre_both[:, :share]
        pre_up_s = pre_both[:, share:]
        activated_s = jax.nn.silu(pre_gate_s)
        hidden_s = (activated_s * pre_up_s).astype(jnp.bfloat16)
        hidden_grad_s = rows_times(grad_p, down_share)
        gate_pre_grad_s = (hidden_grad_s * pre_up_s * silu_grad(pre_gate_s)).astype(jnp.bfloat16)
        up_pre_grad_s = (hidden_grad_s * activated_s).astype(jnp.bfloat16)
        both_p = inner_rows(jnp.concatenate([gate_pre_grad_s, up_pre_grad_s], axis=1), rows_p)
        down_p = inner_rows(hidden_s, grad_p)
        both_sum = both_p if both_sum is None else both_sum + both_p
        down_sum = down_p if down_sum is None else down_sum + down_p
    gate_w_grad = both_sum[:share].astype(jnp.bfloat16)[None]
    up_w_grad = both_sum[share:].astype(jnp.bfloat16)[None]
    down_w_grad = down_sum.astype(jnp.bfloat16)[None]
    part_back, gate_w_grad, up_w_grad, down_w_grad = lax.optimization_barrier(
        (part_back, gate_w_grad, up_w_grad, down_w_grad)
    )
    tokens_grad = matmul(back_pick, part_back).astype(jnp.bfloat16)
    return (layer_out, tokens_grad, gates_grad, gate_w_grad, up_w_grad, down_w_grad)


def solution(mesh):
    return jax.shard_map(
        body,
        mesh=mesh,
        in_specs=(
            P(("rep", "ep"), None),
            P(("rep", "ep"), None),
            P(("rep", "ep"), None),
            P("ep", None, None),
            P("ep", None, None),
            P("ep", None, None),
            P(("rep", "ep"), None),
        ),
        out_specs=(
            P(("rep", "ep"), None),
            P(("rep", "ep"), None),
            P(("rep", "ep"), None),
            P("ep", "rep", None),
            P("ep", "rep", None),
            P("ep", "rep", None),
        ),
        check_vma=False,
    )
```

```python
import jax
import jax.numpy as jnp
from jax import lax
from jax.sharding import PartitionSpec as P

STRIPE = 16


def silu_grad(value):
    sigmoid_value = jax.nn.sigmoid(value)
    return sigmoid_value * (1.0 + value * (1.0 - sigmoid_value))


def rows_times(left, right):
    return lax.dot_general(
        left, right, (((1,), (1,)), ((), ())), preferred_element_type=jnp.float32
    )


def inner_rows(left, right):
    return lax.dot_general(
        left, right, (((0,), (0,)), ((), ())), preferred_element_type=jnp.float32
    )


def matmul(left, right):
    return jnp.dot(left, right, preferred_element_type=jnp.float32)


def body(tokens, expert_ids, gate_weights, w_gate, w_up, w_down, out_grad):
    tok_count, feature_width = tokens.shape
    top_count = expert_ids.shape[1]
    experts = lax.axis_size("ep")
    per_pair = tok_count // 8
    total_slots = experts * per_pair
    live_cols = min(top_count, -(-experts // STRIPE))
    assigned = tok_count * live_cols

    flat_ids = expert_ids[:, :live_cols].reshape(-1)
    flat_gates = gate_weights[:, :live_cols].reshape(-1)
    live_mask = flat_ids < experts
    onehot = flat_ids[:, None] == jnp.arange(experts, dtype=jnp.int32)[None, :]
    position = jnp.arange(assigned, dtype=jnp.int32)
    earlier = (position[:, None] > position[None, :]).astype(jnp.bfloat16)
    before = matmul(earlier, onehot.astype(jnp.bfloat16))
    slot_rank = jnp.sum(jnp.where(onehot, before, 0.0), axis=1).astype(jnp.int32)
    slot_index = jnp.where(live_mask, flat_ids * per_pair + slot_rank, -1)

    slot_ids = jnp.arange(total_slots, dtype=jnp.int32)
    hit = slot_ids[:, None] == slot_index[None, :]
    slot_gate = jnp.sum(jnp.where(hit, flat_gates[None, :], 0.0), axis=1)
    pick = jnp.any(hit.reshape(total_slots, tok_count, live_cols), axis=2).astype(jnp.bfloat16)
    send_rows = matmul(pick, tokens).astype(jnp.bfloat16)
    grad_rows = matmul(pick, out_grad)
    scaled_grad = (slot_gate[:, None] * grad_rows).astype(jnp.bfloat16)

    def exchange(rows):
        return lax.all_to_all(
            rows.reshape(experts, per_pair, feature_width),
            "ep",
            split_axis=0,
            concat_axis=0,
            tiled=True,
        ).reshape(total_slots, feature_width)

    rows_in = exchange(send_rows)
    grad_in = exchange(scaled_grad)

    copies = lax.axis_size("rep")
    by_pieces = copies == 4

    def to_copy(values, step):
        return lax.ppermute(values, "rep", [(r, r ^ step) for r in range(copies)])

    if by_pieces:
        far_rows = to_copy(rows_in, 2)
        near_rows = to_copy(rows_in, 1)
    else:
        gathered_rows = lax.all_gather(rows_in, "rep", axis=0, tiled=True)
        gathered_grad = lax.all_gather(grad_in, "rep", axis=0, tiled=True)

    gate_mat = w_gate[0]
    up_mat = w_up[0]
    down_mat = w_down[0]
    gate_up_mat = jnp.concatenate([gate_mat, up_mat], axis=0)
    hidden_units = gate_mat.shape[0]
    pre_both_own = rows_times(rows_in, gate_up_mat)
    pre_gate = pre_both_own[:, :hidden_units]
    pre_up = pre_both_own[:, hidden_units:]
    activated = jax.nn.silu(pre_gate)
    hidden = (activated * pre_up).astype(jnp.bfloat16)
    expert_out = matmul(hidden, down_mat).astype(jnp.bfloat16)
    expert_out, grad_in = lax.optimization_barrier((expert_out, grad_in))
    returned = lax.all_to_all(
        expert_out.reshape(experts, per_pair, feature_width),
        "ep",
        split_axis=0,
        concat_axis=0,
        tiled=True,
    ).reshape(total_slots, feature_width)

    hidden_grad = rows_times(grad_in, down_mat)
    gate_pre_grad = (hidden_grad * pre_up * silu_grad(pre_gate)).astype(jnp.bfloat16)
    up_pre_grad = (hidden_grad * activated).astype(jnp.bfloat16)
    token_part = matmul(
        jnp.concatenate([gate_pre_grad, up_pre_grad], axis=1), gate_up_mat
    ).astype(jnp.bfloat16)
    if by_pieces:
        token_part, grad_out = lax.optimization_barrier((token_part, grad_in))
        far_grad = to_copy(grad_out, 2)
        near_grad = to_copy(grad_out, 1)
    part_back = lax.all_to_all(
        token_part.reshape(experts, per_pair, feature_width),
        "ep",
        split_axis=0,
        concat_axis=0,
        tiled=True,
    ).reshape(total_slots, feature_width)

    if by_pieces:
        returned, near_rows, near_grad = lax.optimization_barrier((returned, near_rows, near_grad))
    slot_grid = slot_index.reshape(tok_count, live_cols)
    gate_grid = flat_gates.reshape(tok_count, live_cols)
    layer_sum = jnp.zeros((tok_count, feature_width), jnp.float32)
    gate_cols = []
    back_pick = jnp.zeros((tok_count, total_slots), jnp.bfloat16)
    for col in range(live_cols):
        col_pick = (slot_grid[:, col : col + 1] == slot_ids[None, :]).astype(jnp.bfloat16)
        back_pick = back_pick + col_pick
        out_rows = matmul(col_pick, returned)
        layer_sum = layer_sum + gate_grid[:, col : col + 1] * out_rows
        gate_cols.append(jnp.sum(out_grad.astype(jnp.float32) * out_rows, axis=1))
    if by_pieces:
        layer_sum, far_rows, far_grad = lax.optimization_barrier((layer_sum, far_rows, far_grad))
        pieces = [
            (rows_in, grad_in),
            (near_rows, near_grad),
            (far_rows, far_grad),
            (to_copy(far_rows, 1), to_copy(far_grad, 1)),
        ]
    else:
        pieces = [(gathered_rows, gathered_grad)]
    layer_out = layer_sum.astype(jnp.bfloat16)
    gate_cols.extend(
        [jnp.zeros((tok_count,), jnp.float32)] * (top_count - live_cols)
    )
    gates_grad = jnp.stack(gate_cols, axis=1)

    share = gate_mat.shape[0] // copies
    start = lax.axis_index("rep") * share
    gate_share = lax.dynamic_slice_in_dim(gate_mat, start, share, axis=0)
    up_share = lax.dynamic_slice_in_dim(up_mat, start, share, axis=0)
    down_share = lax.dynamic_slice_in_dim(down_mat, start, share, axis=0)
    both_sum = None
    down_sum = None
    stacked_share = jnp.concatenate([gate_share, up_share], axis=0)
    for rows_p, grad_p in pieces:
        pre_both = rows_times(rows_p, stacked_share)
        pre_gate_s = pre_both[:, :share]
        pre_up_s = pre_both[:, share:]
        activated_s = jax.nn.silu(pre_gate_s)
        hidden_s = (activated_s * pre_up_s).astype(jnp.bfloat16)
        hidden_grad_s = rows_times(grad_p, down_share)
        gate_pre_grad_s = (hidden_grad_s * pre_up_s * silu_grad(pre_gate_s)).astype(jnp.bfloat16)
        up_pre_grad_s = (hidden_grad_s * activated_s).astype(jnp.bfloat16)
        both_p = inner_rows(jnp.concatenate([gate_pre_grad_s, up_pre_grad_s], axis=1), rows_p)
        down_p = inner_rows(hidden_s, grad_p)
        both_sum = both_p if both_sum is None else both_sum + both_p
        down_sum = down_p if down_sum is None else down_sum + down_p
    gate_w_grad = both_sum[:share].astype(jnp.bfloat16)[None]
    up_w_grad = both_sum[share:].astype(jnp.bfloat16)[None]
    down_w_grad = down_sum.astype(jnp.bfloat16)[None]
    part_back, gate_w_grad, up_w_grad, down_w_grad = lax.optimization_barrier(
        (part_back, gate_w_grad, up_w_grad, down_w_grad)
    )
    grad_total = jnp.zeros((tok_count, feature_width), jnp.float32)
    for col in range(live_cols):
        source_slot = jnp.where(slot_grid[:, col] < 0, total_slots, slot_grid[:, col])
        grad_total = grad_total + jnp.take(
            part_back, source_slot, axis=0, mode="fill", fill_value=0
        ).astype(jnp.float32)
    tokens_grad = grad_total.astype(jnp.bfloat16)
    return (layer_out, tokens_grad, gates_grad, gate_w_grad, up_w_grad, down_w_grad)


def solution(mesh):
    return jax.shard_map(
        body,
        mesh=mesh,
        in_specs=(
            P(("rep", "ep"), None),
            P(("rep", "ep"), None),
            P(("rep", "ep"), None),
            P("ep", None, None),
            P("ep", None, None),
            P("ep", None, None),
            P(("rep", "ep"), None),
        ),
        out_specs=(
            P(("rep", "ep"), None),
            P(("rep", "ep"), None),
            P(("rep", "ep"), None),
            P("ep", "rep", None),
            P("ep", "rep", None),
            P("ep", "rep", None),
        ),
        check_vma=False,
    )
```

```python
import jax
import jax.numpy as jnp
from jax import lax
from jax.sharding import PartitionSpec as P

STRIPE = 16


def silu_grad(value):
    sigmoid_value = jax.nn.sigmoid(value)
    return sigmoid_value * (1.0 + value * (1.0 - sigmoid_value))


def rows_times(left, right):
    return lax.dot_general(
        left, right, (((1,), (1,)), ((), ())), preferred_element_type=jnp.float32
    )


def inner_rows(left, right):
    return lax.dot_general(
        left, right, (((0,), (0,)), ((), ())), preferred_element_type=jnp.float32
    )


def matmul(left, right):
    return jnp.dot(left, right, preferred_element_type=jnp.float32)


def body(tokens, expert_ids, gate_weights, w_gate, w_up, w_down, out_grad):
    tok_count, feature_width = tokens.shape
    top_count = expert_ids.shape[1]
    experts = lax.axis_size("ep")
    per_pair = tok_count // 8
    total_slots = experts * per_pair
    live_cols = min(top_count, -(-experts // STRIPE))
    assigned = tok_count * live_cols

    flat_ids = expert_ids[:, :live_cols].reshape(-1)
    flat_gates = gate_weights[:, :live_cols].reshape(-1)
    live_mask = flat_ids < experts
    onehot = flat_ids[:, None] == jnp.arange(experts, dtype=jnp.int32)[None, :]
    position = jnp.arange(assigned, dtype=jnp.int32)
    earlier = (position[:, None] > position[None, :]).astype(jnp.bfloat16)
    before = matmul(earlier, onehot.astype(jnp.bfloat16))
    slot_rank = jnp.sum(jnp.where(onehot, before, 0.0), axis=1).astype(jnp.int32)
    slot_index = jnp.where(live_mask, flat_ids * per_pair + slot_rank, -1)

    slot_ids = jnp.arange(total_slots, dtype=jnp.int32)
    hit = slot_ids[:, None] == slot_index[None, :]
    slot_gate = jnp.sum(jnp.where(hit, flat_gates[None, :], 0.0), axis=1)
    pick = jnp.any(hit.reshape(total_slots, tok_count, live_cols), axis=2).astype(jnp.bfloat16)
    send_rows = jnp.dot(pick, tokens, preferred_element_type=jnp.bfloat16)
    grad_rows = matmul(pick, out_grad)
    scaled_grad = (slot_gate[:, None] * grad_rows).astype(jnp.bfloat16)

    def exchange(rows):
        return lax.all_to_all(
            rows.reshape(experts, per_pair, feature_width),
            "ep",
            split_axis=0,
            concat_axis=0,
            tiled=True,
        ).reshape(total_slots, feature_width)

    rows_in = exchange(send_rows)
    grad_in = exchange(scaled_grad)

    copies = lax.axis_size("rep")
    by_pieces = copies == 4

    def to_copy(values, step):
        return lax.ppermute(values, "rep", [(r, r ^ step) for r in range(copies)])

    if by_pieces:
        far_rows = to_copy(rows_in, 2)
        near_rows = to_copy(rows_in, 1)
    else:
        gathered_rows = lax.all_gather(rows_in, "rep", axis=0, tiled=True)
        gathered_grad = lax.all_gather(grad_in, "rep", axis=0, tiled=True)

    gate_mat = w_gate[0]
    up_mat = w_up[0]
    down_mat = w_down[0]
    gate_up_mat = jnp.concatenate([gate_mat, up_mat], axis=0)
    hidden_units = gate_mat.shape[0]
    pre_both_own = rows_times(rows_in, gate_up_mat)
    pre_gate = pre_both_own[:, :hidden_units]
    pre_up = pre_both_own[:, hidden_units:]
    activated = jax.nn.silu(pre_gate)
    hidden = (activated * pre_up).astype(jnp.bfloat16)
    expert_out = matmul(hidden, down_mat).astype(jnp.bfloat16)
    expert_out, grad_in = lax.optimization_barrier((expert_out, grad_in))
    returned = lax.all_to_all(
        expert_out.reshape(experts, per_pair, feature_width),
        "ep",
        split_axis=0,
        concat_axis=0,
        tiled=True,
    ).reshape(total_slots, feature_width)

    hidden_grad = rows_times(grad_in, down_mat)
    gate_pre_grad = (hidden_grad * pre_up * silu_grad(pre_gate)).astype(jnp.bfloat16)
    up_pre_grad = (hidden_grad * activated).astype(jnp.bfloat16)
    token_part = matmul(
        jnp.concatenate([gate_pre_grad, up_pre_grad], axis=1), gate_up_mat
    ).astype(jnp.bfloat16)
    if by_pieces:
        token_part, grad_out = lax.optimization_barrier((token_part, grad_in))
        far_grad = to_copy(grad_out, 2)
        near_grad = to_copy(grad_out, 1)
    part_back = lax.all_to_all(
        token_part.reshape(experts, per_pair, feature_width),
        "ep",
        split_axis=0,
        concat_axis=0,
        tiled=True,
    ).reshape(total_slots, feature_width)

    if by_pieces:
        returned, near_rows, near_grad = lax.optimization_barrier((returned, near_rows, near_grad))
    slot_grid = slot_index.reshape(tok_count, live_cols)
    gate_grid = flat_gates.reshape(tok_count, live_cols)
    layer_sum = jnp.zeros((tok_count, feature_width), jnp.float32)
    gate_cols = []
    back_pick = jnp.zeros((tok_count, total_slots), jnp.bfloat16)
    for col in range(live_cols):
        col_pick = (slot_grid[:, col : col + 1] == slot_ids[None, :]).astype(jnp.bfloat16)
        back_pick = back_pick + col_pick
        out_rows = matmul(col_pick, returned)
        layer_sum = layer_sum + gate_grid[:, col : col + 1] * out_rows
        gate_cols.append(jnp.sum(out_grad.astype(jnp.float32) * out_rows, axis=1))
    if by_pieces:
        layer_sum, far_rows, far_grad = lax.optimization_barrier((layer_sum, far_rows, far_grad))
        pieces = [
            (rows_in, grad_in),
            (near_rows, near_grad),
            (far_rows, far_grad),
            (to_copy(far_rows, 1), to_copy(far_grad, 1)),
        ]
    else:
        pieces = [(gathered_rows, gathered_grad)]
    layer_out = layer_sum.astype(jnp.bfloat16)
    gate_cols.extend(
        [jnp.zeros((tok_count,), jnp.float32)] * (top_count - live_cols)
    )
    gates_grad = jnp.stack(gate_cols, axis=1)

    share = gate_mat.shape[0] // copies
    start = lax.axis_index("rep") * share
    gate_share = lax.dynamic_slice_in_dim(gate_mat, start, share, axis=0)
    up_share = lax.dynamic_slice_in_dim(up_mat, start, share, axis=0)
    down_share = lax.dynamic_slice_in_dim(down_mat, start, share, axis=0)
    both_sum = None
    down_sum = None
    stacked_share = jnp.concatenate([gate_share, up_share], axis=0)
    for rows_p, grad_p in pieces:
        pre_both = rows_times(rows_p, stacked_share)
        pre_gate_s = pre_both[:, :share]
        pre_up_s = pre_both[:, share:]
        activated_s = jax.nn.silu(pre_gate_s)
        hidden_s = (activated_s * pre_up_s).astype(jnp.bfloat16)
        hidden_grad_s = rows_times(grad_p, down_share)
        gate_pre_grad_s = (hidden_grad_s * pre_up_s * silu_grad(pre_gate_s)).astype(jnp.bfloat16)
        up_pre_grad_s = (hidden_grad_s * activated_s).astype(jnp.bfloat16)
        both_p = inner_rows(jnp.concatenate([gate_pre_grad_s, up_pre_grad_s], axis=1), rows_p)
        down_p = inner_rows(hidden_s, grad_p)
        both_sum = both_p if both_sum is None else both_sum + both_p
        down_sum = down_p if down_sum is None else down_sum + down_p
    gate_w_grad = both_sum[:share].astype(jnp.bfloat16)[None]
    up_w_grad = both_sum[share:].astype(jnp.bfloat16)[None]
    down_w_grad = down_sum.astype(jnp.bfloat16)[None]
    part_back, gate_w_grad, up_w_grad, down_w_grad = lax.optimization_barrier(
        (part_back, gate_w_grad, up_w_grad, down_w_grad)
    )
    tokens_grad = jnp.dot(back_pick, part_back, preferred_element_type=jnp.bfloat16)
    return (layer_out, tokens_grad, gates_grad, gate_w_grad, up_w_grad, down_w_grad)


def solution(mesh):
    return jax.shard_map(
        body,
        mesh=mesh,
        in_specs=(
            P(("rep", "ep"), None),
            P(("rep", "ep"), None),
            P(("rep", "ep"), None),
            P("ep", None, None),
            P("ep", None, None),
            P("ep", None, None),
            P(("rep", "ep"), None),
        ),
        out_specs=(
            P(("rep", "ep"), None),
            P(("rep", "ep"), None),
            P(("rep", "ep"), None),
            P("ep", "rep", None),
            P("ep", "rep", None),
            P("ep", "rep", None),
        ),
        check_vma=False,
    )
```
